256 devices in a mesh: blk: 64 (over z_hi, x, y, core), path: 4 (over z_lo).
Axes of the slice: x: 4, y: 4, z: 8 (z_hi: 2, z_lo: 4; z = z_hi * 4 + z_lo), core: 2. Of those that a mesh axis runs over, the one named last changes fastest.
Arguments:
- records: bfloat16 [65536, 512], P('blk'), may hold values from -87.98545 to 87.98545
- coefficients: float32 [65536, 64], P('blk', 'path'), may hold values from -6 to 6
- velocity: float32 [65536, 64], P('blk', 'path'), may hold values from -3 to 3
- targets: float32 [65536, 64], P('blk', 'path'), may hold values from -6 to 6
- block_local: int32 [3, 1536], P(None, 'blk'), may hold values from 0 to 1023
- block_count: int32 [3, 64], replicated, may hold values from 1 to 24, 1024 in all within a row
- candidates: bfloat16 [32768, 512], P('blk'), may hold values from -87.98545 to 87.98545
- frequencies: bfloat16 [512, 1024], replicated, may hold values from -0.25 to 0.25
- phases: float32 [1024], replicated, may hold values from -3.140625 to 3.140625
- prior_weight: float32 [1024, 64], P(None, 'path'), may hold values from -6 to 6
Outputs:
- coefficients_out: float32 [65536, 64], P('blk', 'path')
- velocity_out: float32 [65536, 64], P('blk', 'path')
- scores: float32 [32768, 64], P('blk', 'path')
- path_rms: float32 [32768], P('blk')
The draws below stay inside these ranges and needn't reach their ends.
Inputs may be any that keep to these rules, and one draw needn't show every extreme that they name: `block_count`: each row sums to 1024, and its largest entry is exactly 24. `block_local`: index within the owner's records; a slot at or beyond the owner's count in that step is not used. Used entries of one owner may repeat.
All inputs are finite; a program needn't handle non-finite values.
Results may differ from the reference program's by a relative error of at most 0.0014.
Values may be sent and summed in bfloat16 or wider, within the bound.
No kernel may reach another device: no remote copies, remote signals or barrier semaphores. Data moves between devices by JAX's collectives and lax.ppermute only.
A program may use at most 128 MiB of HBM per device.

```python
import math
import jax
import jax.numpy as jnp
import numpy as np
from jax import lax

D = 512
FEATS = 1024
PATHS = 64
STEPS = 3
REC_DEV = 1024
CAND_DEV = 512
CAP = 24
BLOCK = 1024
RECORDS = 65536
CANDIDATES = 32768
N_BLK = 64


def column_spread(key, power, level):
    order = jax.random.permutation(jax.random.fold_in(key, 4099), D)
    rank = order.astype(jnp.float32)
    return jnp.sqrt(level * D * (rank + 1.0) ** (-power))


def draw_records(key, part):
    spread = column_spread(key, 1.5, 0.42)
    noise = jax.random.truncated_normal(jax.random.fold_in(key, 11), -6.0, 6.0, (RECORDS, D), jnp.float32)
    return (noise * spread[None, :]).astype(jnp.bfloat16)


def draw_candidates(key, part):
    spread = column_spread(key, 1.5, 0.42)
    noise = jax.random.truncated_normal(jax.random.fold_in(key, 12), -6.0, 6.0, (CANDIDATES, D), jnp.float32)
    return (noise * spread[None, :]).astype(jnp.bfloat16)


def plant(values, stream_key, low, top_value):
    place = [jax.random.randint(jax.random.fold_in(stream_key, axis), (), 0, length) for axis, length in enumerate(values.shape)]
    main_axis = values.shape.index(max(values.shape))
    beside = place[:main_axis] + [(place[main_axis] + 1) % values.shape[main_axis]] + place[main_axis + 1:]
    return values.at[tuple(place)].set(low).at[tuple(beside)].set(top_value)


def levels(own_key, extent, pieces, least, top_value):
    loudness, own = 1.0, jax.random.fold_in(own_key, 6)
    for position, parts in pieces:
        steps = jnp.exp(jax.random.uniform(jax.random.fold_in(own, position), (parts,), jnp.float32, least / len(pieces), top_value / len(pieces)))
        loudness = loudness * jnp.repeat(steps, extent[position] // parts).reshape([-1 if axis == position else 1 for axis in range(len(extent))])
    return loudness


def profile(count, total, most, skew):
    loads = [(1 << 20) // math.isqrt(grade ** skew) + 1 for grade in range(2, count + 1)]
    spare, counts = total - most - (count - 1), [1] * (count - 1)
    while spare > 0:
        free = [i for i in range(count - 1) if counts[i] < most]
        pool, left = sum([loads[i] for i in free]), spare
        for i in free:
            extra = min(most - counts[i], max(1, left * loads[i] // pool), spare)
            counts[i] = counts[i] + extra
            spare = spare - extra
    return np.array([most] + counts)


def uneven(key, amount, total, most, slope):
    if amount == 2:
        one = jax.random.randint(key, (), max(1, total - most), min(most, total - 1) + 1)
        return jnp.stack([one, total - one])
    lengths = jnp.asarray(profile(amount, total, most, slope), jnp.int32)
    twos = (amount - 1) // 2
    source_of, sink = lengths[1:1 + 2 * twos:2], lengths[2:2 + 2 * twos:2]
    slack = jnp.minimum(source_of - 1, most - sink)
    moved = jax.random.randint(jax.random.fold_in(key, 1), (twos,), 0, 1 << 20) % (slack + 1)
    lengths = lengths.at[1:1 + 2 * twos:2].set(source_of - moved).at[2:2 + 2 * twos:2].set(sink + moved)
    return lengths[jax.random.permutation(jax.random.fold_in(key, 2), amount)]


def centred(own_key, shape, deviation, limit, split=(), held_as=jnp.bfloat16):
    gain = levels(own_key, shape, split, -0.22, 0.18) if split else 1.0
    values = jax.random.normal(own_key, shape, jnp.float32) * deviation * gain
    return jnp.minimum(jnp.maximum(values, -limit), limit).astype(held_as)


def setup_inputs(seed: int = 0) -> dict:
    arg_keys = jax.random.split(jax.random.key(seed), 11)
    records = draw_records(jax.random.fold_in(arg_keys[10], 71), 0)
    coefficients = centred(arg_keys[1], (RECORDS, PATHS), 1.0, 6.0, ((0, 64), (1, 4)), jnp.float32)
    velocity = centred(arg_keys[2], (RECORDS, PATHS), 0.2, 3.0, ((0, 64), (1, 4)), jnp.float32)
    targets = centred(arg_keys[3], (RECORDS, PATHS), 1.0, 6.0, ((0, 64), (1, 4)), jnp.float32)
    block_local = plant(jax.random.randint(arg_keys[4], (STEPS, N_BLK * CAP), 0, REC_DEV), jax.random.fold_in(arg_keys[4], 1), 0, REC_DEV - 1).astype(jnp.int32)
    block_count = jax.vmap(lambda own: uneven(own, N_BLK, BLOCK, CAP, 2))(jax.random.split(arg_keys[5], STEPS)).reshape((STEPS, N_BLK)).astype(jnp.int32)
    candidates = draw_candidates(jax.random.fold_in(arg_keys[10], 71), 0)
    frequencies = centred(arg_keys[7], (D, FEATS), D ** -0.5, 0.25)
    phases = jnp.clip(jax.random.uniform(arg_keys[8], (FEATS,), jnp.float32, -3.140625, 3.140625), -3.140625, 3.140625)
    prior_weight = centred(arg_keys[9], (FEATS, PATHS), 1.0, 6.0, ((1, 4),), jnp.float32)
    return dict(records=records, coefficients=coefficients, velocity=velocity, targets=targets, block_local=block_local, block_count=block_count, candidates=candidates, frequencies=frequencies, phases=phases, prior_weight=prior_weight)


NOISE = 0.5
MOMENTUM = 0.9
RATE = 0.3
EPSILON = 1e-06
SIGNAL = 9.0

def square_norms(row_block):
    widened = row_block.astype(jnp.float32)
    return lax.optimization_barrier(jnp.sum(widened * widened, axis=1))

def kernel_apply(left_rows, left_norms, right_rows, right_norms, weights):
    dot_values = lax.dot_general(left_rows, right_rows, (((1,), (1,)), ((), ())), preferred_element_type=jnp.float32)
    distance = left_norms[:, None] + right_norms[None, :] - 2.0 * dot_values
    kernel_tile = SIGNAL * jnp.exp(-distance / left_rows.shape[1])
    return jnp.dot(kernel_tile, weights, precision=lax.Precision.HIGHEST)

def prior_values(cand_rows, frequencies, phases, prior_weight):
    angles = jnp.dot(cand_rows, frequencies, preferred_element_type=jnp.float32) * math.sqrt(2.0) + phases[None, :]
    features = math.sqrt(2.0 * SIGNAL / frequencies.shape[1]) * jnp.cos(angles)
    return jnp.dot(features, prior_weight, precision=lax.Precision.HIGHEST)

def all_shards(left_rows, shard_rows, shard_norms, shard_coefs):
    left_norms = square_norms(left_rows)

    def accumulate(running, members):
        return (running + kernel_apply(left_rows, left_norms, members[0], members[1], members[2]), None)
    summed, _ = lax.scan(accumulate, jnp.zeros((left_rows.shape[0], PATHS), jnp.float32), (shard_rows, shard_norms, shard_coefs))
    return summed

def reference(records, coefficients, velocity, targets, block_local, block_count, candidates, frequencies, phases, prior_weight):
    root_count = jnp.sqrt(jnp.float32(RECORDS))
    record_norms = square_norms(records)
    shard_rows = records.reshape(N_BLK, REC_DEV, D)
    shard_norms = record_norms.reshape(N_BLK, REC_DEV)
    owners = jnp.arange(N_BLK, dtype=jnp.int32)[:, None]
    slot_ids = jnp.arange(CAP, dtype=jnp.int32)[None, :]
    for repeat in range(STEPS):
        local_rows = block_local[repeat].reshape(N_BLK, CAP)
        row_index = (owners * REC_DEV + local_rows).reshape(-1).astype(jnp.int32)
        is_live = (slot_ids < block_count[repeat][:, None]).reshape(-1)
        shard_coefs = coefficients.reshape(N_BLK, REC_DEV, PATHS)
        product = all_shards(records[row_index], shard_rows, shard_norms, shard_coefs) / root_count
        gradient = jnp.where(is_live[:, None], product + NOISE * coefficients[row_index] - targets[row_index], 0.0)
        velocity = (MOMENTUM * velocity).at[row_index].add(-RATE * gradient)
        coefficients = coefficients + velocity
    group_rows = candidates.reshape(N_BLK, CAND_DEV, D)
    shard_coefs = coefficients.reshape(N_BLK, REC_DEV, PATHS)

    def group_score(members):
        cand_group, first_rows, first_norms, first_coefs, second_rows, second_norms, second_coefs = members
        group_norms = square_norms(cand_group)
        first_part = prior_values(cand_group, frequencies, phases, prior_weight) + kernel_apply(cand_group, group_norms, first_rows, first_norms, first_coefs) / root_count
        return first_part + kernel_apply(cand_group, group_norms, second_rows, second_norms, second_coefs) / root_count

    def rolled(array_in):
        return jnp.roll(array_in, -1, axis=0)
    per_group = lax.map(group_score, (group_rows, shard_rows, shard_norms, shard_coefs, rolled(shard_rows), rolled(shard_norms), rolled(shard_coefs)))
    scores = jnp.roll(per_group, 2, axis=0).reshape(CANDIDATES, PATHS)
    path_rms = jnp.sqrt(lax.optimization_barrier(jnp.sum(scores * scores, axis=1)) / PATHS + EPSILON)
    return (coefficients, velocity, scores, path_rms)
```

```python
import math

import jax
import jax.numpy as jnp
from jax import lax
from jax.sharding import PartitionSpec as P

NOISE = 0.5
MOMENTUM = 0.9
RATE = 0.3
EPSILON = 1e-06
SIGNAL = 9.0


def passed_along(shard, axis, by):
    length = lax.axis_size(axis)
    return lax.ppermute(shard, axis, [(i, (i + by) % length) for i in range(length)])


def square_norms(row_block):
    widened = row_block.astype(jnp.float32)
    return jnp.sum(widened * widened, axis=1)


def kernel_apply(left_rows, left_norms, right_rows, right_norms, weights):
    dot_values = lax.dot_general(
        left_rows, right_rows, (((1,), (1,)), ((), ())), preferred_element_type=jnp.float32
    )
    distance = left_norms[:, None] + right_norms[None, :] - 2.0 * dot_values
    kernel_tile = SIGNAL * jnp.exp(-distance / left_rows.shape[1])
    return jnp.dot(kernel_tile, weights, precision=lax.Precision.HIGHEST)


def prior_values(cand_rows, frequencies, phases, prior_weight):
    angles = (
        jnp.dot(cand_rows, frequencies, preferred_element_type=jnp.float32) * math.sqrt(2.0)
        + phases[None, :]
    )
    features = math.sqrt(2.0 * SIGNAL / frequencies.shape[1]) * jnp.cos(angles)
    return jnp.dot(features, prior_weight, precision=lax.Precision.HIGHEST)


def gather_blocks(block, axis):
    length = lax.axis_size(axis)
    flat = block.reshape(1, -1)
    spread = jnp.broadcast_to(flat, (length, flat.shape[1]))
    got = lax.all_to_all(spread, axis, 0, 0, tiled=True)
    return got.reshape((length,) + block.shape)


def sum_to_owners(partial, axis):
    length = lax.axis_size(axis)
    flat = partial.reshape(length, -1)
    got = lax.all_to_all(flat, axis, 0, 0, tiled=True)
    return jnp.sum(got, axis=0).reshape(partial.shape[1:])


def velocity_weights(steps):
    a, b = [], []
    for t in range(steps):
        a.append(sum(MOMENTUM ** u for u in range(1, t + 1)))
        b.append([sum(MOMENTUM ** (u - 1 - s) for u in range(s + 1, t + 1)) for s in range(t)])
    return a, b


def shards(
    records,
    coefficients,
    velocity,
    targets,
    block_local,
    block_count,
    candidates,
    frequencies,
    phases,
    prior_weight,
):
    n_blk = lax.axis_size("blk")
    record_total = records.shape[0] * n_blk
    root_count = jnp.sqrt(jnp.float32(record_total))
    steps, slot_count = block_local.shape
    own_index = lax.axis_index("blk")
    neighbour = passed_along(candidates, "blk", 1)
    work_norms = square_norms(records)
    slot_ids = jnp.arange(slot_count, dtype=jnp.int32)
    paths = coefficients.shape[1]

    own_rows = records[block_local.reshape(-1)]
    gathered = lax.all_gather(own_rows, "blk", axis=0, tiled=False)
    all_rows = gathered.reshape(n_blk * steps * slot_count, -1)
    step_rows = [
        gathered[:, t * slot_count:(t + 1) * slot_count].reshape(n_blk * slot_count, -1)
        for t in range(steps)
    ]
    step_norms = [square_norms(rows) for rows in step_rows]

    start_weights = jnp.concatenate([coefficients, velocity], axis=1)
    partial = kernel_apply(all_rows, square_norms(all_rows), records, work_norms, start_weights)
    start_sums = sum_to_owners(partial.reshape(n_blk, steps * slot_count, 2 * paths), "blk")
    start_sums = start_sums.reshape(steps, slot_count, 2 * paths)

    a_weight, b_weight = velocity_weights(steps)
    updates = []
    for repeat in range(steps):
        local_rows = block_local[repeat]
        own_count = lax.dynamic_index_in_dim(block_count[repeat], own_index, 0, keepdims=False)
        is_live = slot_ids < own_count
        mine = own_rows[repeat * slot_count:(repeat + 1) * slot_count]
        mine_norms = square_norms(mine)
        total = start_sums[repeat, :, :paths]
        if repeat > 0:
            total = total + a_weight[repeat] * start_sums[repeat, :, paths:]
        for earlier in range(repeat):
            cross = kernel_apply(
                mine, mine_norms, step_rows[earlier], step_norms[earlier], updates[earlier]
            )
            total = total + b_weight[repeat][earlier] * cross
        product = total / root_count
        gradient = jnp.where(
            is_live[:, None], product + NOISE * coefficients[local_rows] - targets[local_rows], 0.0
        )
        step_update = -RATE * gradient
        velocity = (MOMENTUM * velocity).at[local_rows].add(step_update)
        coefficients = coefficients + velocity
        if repeat < steps - 1:
            updates.append(gather_blocks(step_update, "blk").reshape(n_blk * slot_count, paths))

    own_sum = kernel_apply(candidates, square_norms(candidates), records, work_norms, coefficients)
    next_sum = kernel_apply(neighbour, square_norms(neighbour), records, work_norms, coefficients)
    first_part = prior_values(candidates, frequencies, phases, prior_weight) + own_sum / root_count
    next_term = next_sum / root_count
    scores = passed_along(first_part, "blk", 2) + passed_along(next_term, "blk", 1)
    squares_local = jnp.sum(scores * scores, axis=1)
    summed = lax.psum(squares_local, "path")
    path_rms = jnp.sqrt(summed / (scores.shape[1] * lax.axis_size("path")) + EPSILON)
    return (coefficients, velocity, scores, path_rms)


def solution(mesh):
    return jax.shard_map(
        shards,
        mesh=mesh,
        in_specs=(
            P("blk", None),
            P("blk", "path"),
            P("blk", "path"),
            P("blk", "path"),
            P(None, "blk"),
            P(),
            P("blk", None),
            P(),
            P(),
            P(None, "path"),
        ),
        out_specs=(P("blk", "path"), P("blk", "path"), P("blk", "path"), P("blk")),
        check_vma=False,
    )
```

```python
import math

import jax
import jax.numpy as jnp
from jax import lax
from jax.sharding import PartitionSpec as P

NOISE = 0.5
MOMENTUM = 0.9
RATE = 0.3
EPSILON = 1e-06
SIGNAL = 9.0


def passed_along(shard, axis, by):
    length = lax.axis_size(axis)
    return lax.ppermute(shard, axis, [(i, (i + by) % length) for i in range(length)])


def square_norms(row_block):
    widened = row_block.astype(jnp.float32)
    return jnp.sum(widened * widened, axis=1)


def kernel_tile_of(left_rows, left_norms, right_rows, right_norms):
    dot_values = lax.dot_general(
        left_rows, right_rows, (((1,), (1,)), ((), ())), preferred_element_type=jnp.float32
    )
    distance = left_norms[:, None] + right_norms[None, :] - 2.0 * dot_values
    return SIGNAL * jnp.exp(-distance / left_rows.shape[1])


def kernel_apply(left_rows, left_norms, right_rows, right_norms, weights):
    kernel_tile = kernel_tile_of(left_rows, left_norms, right_rows, right_norms)
    return jnp.dot(kernel_tile, weights, precision=lax.Precision.HIGH)


def prior_values(cand_rows, frequencies, phases, prior_weight):
    angles = (
        jnp.dot(cand_rows, frequencies, preferred_element_type=jnp.float32) * math.sqrt(2.0)
        + phases[None, :]
    )
    features = math.sqrt(2.0 * SIGNAL / frequencies.shape[1]) * jnp.cos(angles)
    return jnp.dot(features, prior_weight, precision=lax.Precision.HIGHEST)


def gather_blocks(block, axis):
    length = lax.axis_size(axis)
    flat = block.reshape(1, -1)
    spread = jnp.broadcast_to(flat, (length, flat.shape[1]))
    got = lax.all_to_all(spread, axis, 0, 0, tiled=True)
    return got.reshape((length,) + block.shape)


def sum_to_owners(partial, axis):
    length = lax.axis_size(axis)
    flat = partial.reshape(length, -1)
    got = lax.all_to_all(flat, axis, 0, 0, tiled=True)
    return jnp.sum(got, axis=0).reshape(partial.shape[1:])


def velocity_weights(steps):
    a, b = [], []
    for t in range(steps):
        a.append(sum(MOMENTUM ** u for u in range(1, t + 1)))
        b.append([sum(MOMENTUM ** (u - 1 - s) for u in range(s + 1, t + 1)) for s in range(t)])
    return a, b


def shards(
    records,
    coefficients,
    velocity,
    targets,
    block_local,
    block_count,
    candidates,
    frequencies,
    phases,
    prior_weight,
):
    n_blk = lax.axis_size("blk")
    record_total = records.shape[0] * n_blk
    root_count = jnp.sqrt(jnp.float32(record_total))
    steps, slot_count = block_local.shape
    own_index = lax.axis_index("blk")
    neighbour = passed_along(candidates, "blk", 1)
    work_norms = square_norms(records)
    slot_ids = jnp.arange(slot_count, dtype=jnp.int32)
    paths = coefficients.shape[1]

    own_rows = records[block_local.reshape(-1)]
    gathered = lax.all_gather(own_rows, "blk", axis=0, tiled=False)
    all_rows = gathered.reshape(n_blk * steps * slot_count, -1)
    step_rows = [
        gathered[:, t * slot_count:(t + 1) * slot_count].reshape(n_blk * slot_count, -1)
        for t in range(steps)
    ]
    step_norms = [square_norms(rows) for rows in step_rows]

    start_weights = jnp.concatenate([coefficients, velocity], axis=1)
    partial = kernel_apply(all_rows, square_norms(all_rows), records, work_norms, start_weights)
    start_sums = sum_to_owners(partial.reshape(n_blk, steps * slot_count, 2 * paths), "blk")
    start_sums = start_sums.reshape(steps, slot_count, 2 * paths)

    a_weight, b_weight = velocity_weights(steps + 1)
    own_rows_norms = square_norms(own_rows)
    cand_norms = square_norms(candidates)
    neighbour_norms = square_norms(neighbour)
    own_start = kernel_apply(candidates, cand_norms, records, work_norms, start_weights)
    next_start = kernel_apply(neighbour, neighbour_norms, records, work_norms, start_weights)
    own_slots = kernel_tile_of(candidates, cand_norms, own_rows, own_rows_norms)
    next_slots = kernel_tile_of(neighbour, neighbour_norms, own_rows, own_rows_norms)
    weighted_updates = []
    updates = []
    for repeat in range(steps):
        local_rows = block_local[repeat]
        own_count = lax.dynamic_index_in_dim(block_count[repeat], own_index, 0, keepdims=False)
        is_live = slot_ids < own_count
        mine = own_rows[repeat * slot_count:(repeat + 1) * slot_count]
        mine_norms = square_norms(mine)
        total = start_sums[repeat, :, :paths]
        if repeat > 0:
            total = total + a_weight[repeat] * start_sums[repeat, :, paths:]
        for earlier in range(repeat):
            cross = kernel_apply(
                mine, mine_norms, step_rows[earlier], step_norms[earlier], updates[earlier]
            )
            total = total + b_weight[repeat][earlier] * cross
        product = total / root_count
        gradient = jnp.where(
            is_live[:, None], product + NOISE * coefficients[local_rows] - targets[local_rows], 0.0
        )
        step_update = -RATE * gradient
        velocity = (MOMENTUM * velocity).at[local_rows].add(step_update)
        coefficients = coefficients + velocity
        weighted_updates.append(b_weight[steps][repeat] * step_update)
        if repeat < steps - 1:
            updates.append(gather_blocks(step_update, "blk").reshape(n_blk * slot_count, paths))

    slot_weights = jnp.concatenate(weighted_updates, axis=0)
    own_sum = (
        own_start[:, :paths]
        + a_weight[steps] * own_start[:, paths:]
        + jnp.dot(own_slots, slot_weights, precision=lax.Precision.HIGH)
    )
    next_sum = (
        next_start[:, :paths]
        + a_weight[steps] * next_start[:, paths:]
        + jnp.dot(next_slots, slot_weights, precision=lax.Precision.HIGH)
    )
    first_part = prior_values(candidates, frequencies, phases, prior_weight) + own_sum / root_count
    next_term = next_sum / root_count
    scores = passed_along(first_part, "blk", 2) + passed_along(next_term, "blk", 1)
    squares_local = jnp.sum(scores * scores, axis=1)
    summed = lax.psum(squares_local, "path")
    path_rms = jnp.sqrt(summed / (scores.shape[1] * lax.axis_size("path")) + EPSILON)
    return (coefficients, velocity, scores, path_rms)


def solution(mesh):
    return jax.shard_map(
        shards,
        mesh=mesh,
        in_specs=(
            P("blk", None),
            P("blk", "path"),
            P("blk", "path"),
            P("blk", "path"),
            P(None, "blk"),
            P(),
            P("blk", None),
            P(),
            P(),
            P(None, "path"),
        ),
        out_specs=(P("blk", "path"), P("blk", "path"), P("blk", "path"), P("blk")),
        check_vma=False,
    )
```

```python
import math

import jax
import jax.numpy as jnp
from jax import lax
from jax.sharding import PartitionSpec as P

NOISE = 0.5
MOMENTUM = 0.9
RATE = 0.3
EPSILON = 1e-06
SIGNAL = 9.0


def passed_along(shard, axis, by):
    length = lax.axis_size(axis)
    return lax.ppermute(shard, axis, [(i, (i + by) % length) for i in range(length)])


def square_norms(row_block):
    widened = row_block.astype(jnp.float32)
    return jnp.sum(widened * widened, axis=1)


def kernel_tile_of(left_rows, left_norms, right_rows, right_norms):
    dot_values = lax.dot_general(
        left_rows, right_rows, (((1,), (1,)), ((), ())), preferred_element_type=jnp.float32
    )
    distance = left_norms[:, None] + right_norms[None, :] - 2.0 * dot_values
    return SIGNAL * jnp.exp(-distance / left_rows.shape[1])


def kernel_apply(left_rows, left_norms, right_rows, right_norms, weights):
    kernel_tile = kernel_tile_of(left_rows, left_norms, right_rows, right_norms)
    return jnp.dot(kernel_tile, weights, precision=lax.Precision.HIGH)


def prior_values(cand_rows, frequencies, phases, prior_weight):
    angles = (
        jnp.dot(cand_rows, frequencies, preferred_element_type=jnp.float32) * math.sqrt(2.0)
        + phases[None, :]
    )
    features = math.sqrt(2.0 * SIGNAL / frequencies.shape[1]) * jnp.cos(angles)
    return jnp.dot(features, prior_weight, precision=lax.Precision.HIGHEST)


def gather_blocks(block, axis):
    length = lax.axis_size(axis)
    flat = block.reshape(1, -1)
    spread = jnp.broadcast_to(flat, (length, flat.shape[1]))
    got = lax.all_to_all(spread, axis, 0, 0, tiled=True)
    return got.reshape((length,) + block.shape)


def sum_to_owners(partial, axis):
    length = lax.axis_size(axis)
    flat = partial.reshape(length, -1)
    got = lax.all_to_all(flat, axis, 0, 0, tiled=True)
    return jnp.sum(got, axis=0).reshape(partial.shape[1:])


def velocity_weights(steps):
    a, b = [], []
    for t in range(steps):
        a.append(sum(MOMENTUM ** u for u in range(1, t + 1)))
        b.append([sum(MOMENTUM ** (u - 1 - s) for u in range(s + 1, t + 1)) for s in range(t)])
    return a, b


def shards(
    records,
    coefficients,
    velocity,
    targets,
    block_local,
    block_count,
    candidates,
    frequencies,
    phases,
    prior_weight,
):
    n_blk = lax.axis_size("blk")
    record_total = records.shape[0] * n_blk
    root_count = jnp.sqrt(jnp.float32(record_total))
    steps, slot_count = block_local.shape
    own_index = lax.axis_index("blk")
    neighbour = passed_along(candidates, "blk", 1)
    work_norms = square_norms(records)
    slot_ids = jnp.arange(slot_count, dtype=jnp.int32)
    paths = coefficients.shape[1]

    n_path = lax.axis_size("path")
    path_index = lax.axis_index("path")
    share = slot_count // n_path
    own_rows = records[block_local.reshape(-1)]
    prior = prior_values(candidates, frequencies, phases, prior_weight)

    share_local = lax.dynamic_slice_in_dim(block_local, path_index * share, share, axis=1)
    share_rows = records[share_local.reshape(-1)]
    gathered = gather_blocks(share_rows, "blk")
    gathered, prior = lax.optimization_barrier((gathered, prior))
    all_rows = gathered.reshape(n_blk * steps * share, -1)
    start_weights = jnp.concatenate([coefficients, velocity], axis=1)
    every_weights = lax.all_gather(start_weights, "path", axis=1, tiled=True)
    partial = kernel_apply(all_rows, square_norms(all_rows), records, work_norms, every_weights)
    share_sums = sum_to_owners(partial.reshape(n_blk, steps * share, n_path * 2 * paths), "blk")
    share_sums = share_sums.reshape(steps * share, n_path, 2 * paths).transpose(1, 0, 2)
    got = lax.all_to_all(share_sums, "path", 0, 0, tiled=True)
    start_sums = got.reshape(n_path, steps, share, 2 * paths).transpose(1, 0, 2, 3)
    start_sums = start_sums.reshape(steps, slot_count, 2 * paths)

    pairs = [(t, s) for t in range(steps) for s in range(t)]
    tiles = []
    for t, s in pairs:
        mine = own_rows[t * slot_count:(t + 1) * slot_count]
        theirs = gathered[:, s * share:(s + 1) * share].reshape(n_blk * share, -1)
        tiles.append(kernel_tile_of(mine, square_norms(mine), theirs, square_norms(theirs)))
    tiles = lax.all_gather(jnp.stack(tiles), "path", axis=0, tiled=False)
    tiles = tiles.reshape(n_path, len(pairs), slot_count, n_blk, share).transpose(1, 2, 3, 0, 4)
    tiles = tiles.reshape(len(pairs), slot_count, n_blk * slot_count)
    tile_of = {pair: tiles[k] for k, pair in enumerate(pairs)}

    a_weight, b_weight = velocity_weights(steps + 1)
    own_rows_norms = square_norms(own_rows)
    cand_norms = square_norms(candidates)
    neighbour_norms = square_norms(neighbour)
    own_start = kernel_apply(candidates, cand_norms, records, work_norms, start_weights)
    next_start = kernel_apply(neighbour, neighbour_norms, records, work_norms, start_weights)
    own_slots = kernel_tile_of(candidates, cand_norms, own_rows, own_rows_norms)
    next_slots = kernel_tile_of(neighbour, neighbour_norms, own_rows, own_rows_norms)
    weighted_updates = []
    updates = []
    for repeat in range(steps):
        local_rows = block_local[repeat]
        own_count = lax.dynamic_index_in_dim(block_count[repeat], own_index, 0, keepdims=False)
        is_live = slot_ids < own_count
        total = start_sums[repeat, :, :paths]
        if repeat > 0:
            total = total + a_weight[repeat] * start_sums[repeat, :, paths:]
        for earlier in range(repeat):
            cross = jnp.dot(
                tile_of[(repeat, earlier)], updates[earlier], precision=lax.Precision.HIGH
            )
            total = total + b_weight[repeat][earlier] * cross
        product = total / root_count
        gradient = jnp.where(
            is_live[:, None], product + NOISE * coefficients[local_rows] - targets[local_rows], 0.0
        )
        step_update = -RATE * gradient
        velocity = (MOMENTUM * velocity).at[local_rows].add(step_update)
        coefficients = coefficients + velocity
        weighted_updates.append(b_weight[steps][repeat] * step_update)
        if repeat < steps - 1:
            updates.append(gather_blocks(step_update, "blk").reshape(n_blk * slot_count, paths))

    slot_weights = jnp.concatenate(weighted_updates, axis=0)
    own_sum = (
        own_start[:, :paths]
        + a_weight[steps] * own_start[:, paths:]
        + jnp.dot(own_slots, slot_weights, precision=lax.Precision.HIGH)
    )
    next_sum = (
        next_start[:, :paths]
        + a_weight[steps] * next_start[:, paths:]
        + jnp.dot(next_slots, slot_weights, precision=lax.Precision.HIGH)
    )
    first_part = prior + own_sum / root_count
    next_term = next_sum / root_count
    scores = passed_along(first_part, "blk", 2) + passed_along(next_term, "blk", 1)
    squares_local = jnp.sum(scores * scores, axis=1)
    summed = lax.psum(squares_local, "path")
    path_rms = jnp.sqrt(summed / (scores.shape[1] * lax.axis_size("path")) + EPSILON)
    return (coefficients, velocity, scores, path_rms)


def solution(mesh):
    return jax.shard_map(
        shards,
        mesh=mesh,
        in_specs=(
            P("blk", None),
            P("blk", "path"),
            P("blk", "path"),
            P("blk", "path"),
            P(None, "blk"),
            P(),
            P("blk", None),
            P(),
            P(),
            P(None, "path"),
        ),
        out_specs=(P("blk", "path"), P("blk", "path"), P("blk", "path"), P("blk")),
        check_vma=False,
    )
```

```python
import math

import jax
import jax.numpy as jnp
from jax import lax
from jax.sharding import PartitionSpec as P

NOISE = 0.5
MOMENTUM = 0.9
RATE = 0.3
EPSILON = 1e-06
SIGNAL = 9.0


def passed_along(shard, axis, by):
    length = lax.axis_size(axis)
    return lax.ppermute(shard, axis, [(i, (i + by) % length) for i in range(length)])


def square_norms(row_block):
    widened = row_block.astype(jnp.float32)
    return jnp.sum(widened * widened, axis=1)


def kernel_tile_of(left_rows, left_norms, right_rows, right_norms):
    dot_values = lax.dot_general(
        left_rows, right_rows, (((1,), (1,)), ((), ())), preferred_element_type=jnp.float32
    )
    distance = left_norms[:, None] + right_norms[None, :] - 2.0 * dot_values
    return SIGNAL * jnp.exp(-distance / left_rows.shape[1])


def kernel_apply(left_rows, left_norms, right_rows, right_norms, weights):
    kernel_tile = kernel_tile_of(left_rows, left_norms, right_rows, right_norms)
    return jnp.dot(kernel_tile, weights, precision=lax.Precision.HIGH)


def prior_values(cand_rows, frequencies, phases, prior_weight):
    angles = (
        jnp.dot(cand_rows, frequencies, preferred_element_type=jnp.float32) * math.sqrt(2.0)
        + phases[None, :]
    )
    features = math.sqrt(2.0 * SIGNAL / frequencies.shape[1]) * jnp.cos(angles)
    return jnp.dot(features, prior_weight, precision=lax.Precision.HIGHEST)


def gather_blocks(block, axis):
    length = lax.axis_size(axis)
    flat = block.reshape(1, -1)
    spread = jnp.broadcast_to(flat, (length, flat.shape[1]))
    got = lax.all_to_all(spread, axis, 0, 0, tiled=True)
    return got.reshape((length,) + block.shape)


def gather_stack(block, axis):
    length = lax.axis_size(axis)
    spread = jnp.broadcast_to(block[None], (length,) + block.shape)
    return lax.all_to_all(spread, axis, 0, 0, tiled=True)


def gather_by_permutes(block, axis):
    length = lax.axis_size(axis)
    here = lax.axis_index(axis)
    moved = [block] + [passed_along(block, axis, by) for by in range(1, length)]
    order = (here - jnp.arange(length, dtype=jnp.int32)) % length
    return jnp.take(jnp.stack(moved), order, axis=0)


def sum_to_owners(partial, axis):
    length = lax.axis_size(axis)
    flat = partial.reshape(length, -1)
    got = lax.all_to_all(flat, axis, 0, 0, tiled=True)
    return jnp.sum(got, axis=0).reshape(partial.shape[1:])


def velocity_weights(steps):
    a, b = [], []
    for t in range(steps):
        a.append(sum(MOMENTUM ** u for u in range(1, t + 1)))
        b.append([sum(MOMENTUM ** (u - 1 - s) for u in range(s + 1, t + 1)) for s in range(t)])
    return a, b


def shards(
    records,
    coefficients,
    velocity,
    targets,
    block_local,
    block_count,
    candidates,
    frequencies,
    phases,
    prior_weight,
):
    n_blk = lax.axis_size("blk")
    record_total = records.shape[0] * n_blk
    root_count = jnp.sqrt(jnp.float32(record_total))
    steps, slot_count = block_local.shape
    own_index = lax.axis_index("blk")
    neighbour = passed_along(candidates, "blk", 1)
    work_norms = square_norms(records)
    slot_ids = jnp.arange(slot_count, dtype=jnp.int32)
    paths = coefficients.shape[1]

    n_path = lax.axis_size("path")
    path_index = lax.axis_index("path")
    share = slot_count // n_path
    own_rows = records[block_local.reshape(-1)]
    prior = prior_values(candidates, frequencies, phases, prior_weight)

    share_local = lax.dynamic_slice_in_dim(block_local, path_index * share, share, axis=1)
    share_rows = records[share_local.reshape(-1)]
    gathered = gather_stack(share_rows, "blk")
    gathered, prior = lax.optimization_barrier((gathered, prior))
    all_rows = gathered.reshape(n_blk * steps * share, -1)
    start_weights = jnp.concatenate([coefficients, velocity], axis=1)
    every_weights = gather_by_permutes(start_weights, "path").transpose(1, 0, 2)
    every_weights = every_weights.reshape(start_weights.shape[0], n_path * 2 * paths)
    partial = kernel_apply(all_rows, square_norms(all_rows), records, work_norms, every_weights)
    share_sums = sum_to_owners(partial.reshape(n_blk, steps * share, n_path * 2 * paths), "blk")
    share_sums = share_sums.reshape(steps * share, n_path, 2 * paths).transpose(1, 0, 2)
    got = lax.all_to_all(share_sums, "path", 0, 0, tiled=True)
    start_sums = got.reshape(n_path, steps, share, 2 * paths).transpose(1, 0, 2, 3)
    start_sums = start_sums.reshape(steps, slot_count, 2 * paths)

    pairs = [(t, s) for t in range(steps) for s in range(t)]
    tiles = []
    for t, s in pairs:
        mine = own_rows[t * slot_count:(t + 1) * slot_count]
        theirs = gathered[:, s * share:(s + 1) * share].reshape(n_blk * share, -1)
        tiles.append(kernel_tile_of(mine, square_norms(mine), theirs, square_norms(theirs)))
    tiles = gather_by_permutes(jnp.stack(tiles), "path")
    tiles = tiles.reshape(n_path, len(pairs), slot_count, n_blk, share).transpose(1, 2, 3, 0, 4)
    tiles = tiles.reshape(len(pairs), slot_count, n_blk * slot_count)
    tile_of = {pair: tiles[k] for k, pair in enumerate(pairs)}

    a_weight, b_weight = velocity_weights(steps + 1)
    own_rows_norms = square_norms(own_rows)
    cand_norms = square_norms(candidates)
    neighbour_norms = square_norms(neighbour)
    own_start = kernel_apply(candidates, cand_norms, records, work_norms, start_weights)
    next_start = kernel_apply(neighbour, neighbour_norms, records, work_norms, start_weights)
    own_slots = kernel_tile_of(candidates, cand_norms, own_rows, own_rows_norms)
    next_slots = kernel_tile_of(neighbour, neighbour_norms, own_rows, own_rows_norms)
    weighted_updates = []
    updates = []
    for repeat in range(steps):
        local_rows = block_local[repeat]
        own_count = lax.dynamic_index_in_dim(block_count[repeat], own_index, 0, keepdims=False)
        is_live = slot_ids < own_count
        total = start_sums[repeat, :, :paths]
        if repeat > 0:
            total = total + a_weight[repeat] * start_sums[repeat, :, paths:]
        for earlier in range(repeat):
            cross = jnp.dot(
                tile_of[(repeat, earlier)], updates[earlier], precision=lax.Precision.HIGH
            )
            total = total + b_weight[repeat][earlier] * cross
        product = total / root_count
        gradient = jnp.where(
            is_live[:, None], product + NOISE * coefficients[local_rows] - targets[local_rows], 0.0
        )
        step_update = -RATE * gradient
        velocity = (MOMENTUM * velocity).at[local_rows].add(step_update)
        coefficients = coefficients + velocity
        weighted_updates.append(b_weight[steps][repeat] * step_update)
        if repeat < steps - 1:
            updates.append(gather_blocks(step_update, "blk").reshape(n_blk * slot_count, paths))

    slot_weights = jnp.concatenate(weighted_updates, axis=0)
    own_sum = (
        own_start[:, :paths]
        + a_weight[steps] * own_start[:, paths:]
        + jnp.dot(own_slots, slot_weights, precision=lax.Precision.HIGH)
    )
    next_sum = (
        next_start[:, :paths]
        + a_weight[steps] * next_start[:, paths:]
        + jnp.dot(next_slots, slot_weights, precision=lax.Precision.HIGH)
    )
    first_part = prior + own_sum / root_count
    next_term = next_sum / root_count
    scores = passed_along(first_part, "blk", 2) + passed_along(next_term, "blk", 1)
    squares_local = jnp.sum(scores * scores, axis=1)
    summed = lax.psum(squares_local, "path")
    path_rms = jnp.sqrt(summed / (scores.shape[1] * lax.axis_size("path")) + EPSILON)
    return (coefficients, velocity, scores, path_rms)


def solution(mesh):
    return jax.shard_map(
        shards,
        mesh=mesh,
        in_specs=(
            P("blk", None),
            P("blk", "path"),
            P("blk", "path"),
            P("blk", "path"),
            P(None, "blk"),
            P(),
            P("blk", None),
            P(),
            P(),
            P(None, "path"),
        ),
        out_specs=(P("blk", "path"), P("blk", "path"), P("blk", "path"), P("blk")),
        check_vma=False,
    )
```

```python
import math

import jax
import jax.numpy as jnp
from jax import lax
from jax.sharding import PartitionSpec as P

NOISE = 0.5
MOMENTUM = 0.9
RATE = 0.3
EPSILON = 1e-06
SIGNAL = 9.0


def passed_along(shard, axis, by):
    length = lax.axis_size(axis)
    return lax.ppermute(shard, axis, [(i, (i + by) % length) for i in range(length)])


def square_norms(row_block):
    widened = row_block.astype(jnp.float32)
    return jnp.sum(widened * widened, axis=1)


def kernel_tile_of(left_rows, left_norms, right_rows, right_norms):
    dot_values = lax.dot_general(
        left_rows, right_rows, (((1,), (1,)), ((), ())), preferred_element_type=jnp.float32
    )
    distance = left_norms[:, None] + right_norms[None, :] - 2.0 * dot_values
    return SIGNAL * jnp.exp(-distance / left_rows.shape[1])


def kernel_apply(left_rows, left_norms, right_rows, right_norms, weights):
    kernel_tile = kernel_tile_of(left_rows, left_norms, right_rows, right_norms)
    return jnp.dot(kernel_tile, weights, precision=lax.Precision.HIGH)


def prior_values(cand_rows, frequencies, phases, prior_weight):
    angles = (
        jnp.dot(cand_rows, frequencies, preferred_element_type=jnp.float32) * math.sqrt(2.0)
        + phases[None, :]
    )
    features = math.sqrt(2.0 * SIGNAL / frequencies.shape[1]) * jnp.cos(angles)
    return jnp.dot(features, prior_weight, precision=lax.Precision.HIGHEST)


def gather_blocks(block, axis):
    length = lax.axis_size(axis)
    flat = block.reshape(1, -1)
    spread = jnp.broadcast_to(flat, (length, flat.shape[1]))
    got = lax.all_to_all(spread, axis, 0, 0, tiled=True)
    return got.reshape((length,) + block.shape)


def gather_stack(block, axis):
    length = lax.axis_size(axis)
    spread = jnp.broadcast_to(block[None], (length,) + block.shape)
    return lax.all_to_all(spread, axis, 0, 0, tiled=True)


def gather_by_permutes(block, axis):
    length = lax.axis_size(axis)
    here = lax.axis_index(axis)
    moved = [block] + [passed_along(block, axis, by) for by in range(1, length)]
    order = (here - jnp.arange(length, dtype=jnp.int32)) % length
    return jnp.take(jnp.stack(moved), order, axis=0)


def sum_to_owners(partial, axis):
    length = lax.axis_size(axis)
    flat = partial.reshape(length, -1)
    got = lax.all_to_all(flat, axis, 0, 0, tiled=True)
    return jnp.sum(got, axis=0).reshape(partial.shape[1:])


def velocity_weights(steps):
    a, b = [], []
    for t in range(steps):
        a.append(sum(MOMENTUM ** u for u in range(1, t + 1)))
        b.append([sum(MOMENTUM ** (u - 1 - s) for u in range(s + 1, t + 1)) for s in range(t)])
    return a, b


def shards(
    records,
    coefficients,
    velocity,
    targets,
    block_local,
    block_count,
    candidates,
    frequencies,
    phases,
    prior_weight,
):
    n_blk = lax.axis_size("blk")
    record_total = records.shape[0] * n_blk
    root_count = jnp.sqrt(jnp.float32(record_total))
    steps, slot_count = block_local.shape
    own_index = lax.axis_index("blk")
    neighbour = passed_along(candidates, "blk", 1)
    work_norms = square_norms(records)
    slot_ids = jnp.arange(slot_count, dtype=jnp.int32)
    paths = coefficients.shape[1]

    n_path = lax.axis_size("path")
    path_index = lax.axis_index("path")
    share = slot_count // n_path
    own_rows = records[block_local.reshape(-1)]
    prior = prior_values(candidates, frequencies, phases, prior_weight)

    share_local = lax.dynamic_slice_in_dim(block_local, path_index * share, share, axis=1)
    share_rows = records[share_local.reshape(-1)]
    gathered = gather_stack(share_rows, "blk")
    gathered, prior = lax.optimization_barrier((gathered, prior))
    all_rows = gathered.reshape(n_blk * steps * share, -1)
    pairs = [(t, s) for t in range(steps) for s in range(t)]
    tiles = []
    for t, s in pairs:
        mine = own_rows[t * slot_count:(t + 1) * slot_count]
        theirs = gathered[:, s * share:(s + 1) * share].reshape(n_blk * share, -1)
        tiles.append(kernel_tile_of(mine, square_norms(mine), theirs, square_norms(theirs)))
    tiles = jnp.stack(tiles)
    tiles, all_rows = lax.optimization_barrier((tiles, all_rows))
    tiles = gather_by_permutes(tiles, "path")
    tiles = tiles.reshape(n_path, len(pairs), slot_count, n_blk, share).transpose(1, 2, 3, 0, 4)
    tiles = tiles.reshape(len(pairs), slot_count, n_blk * slot_count)
    tile_of = {pair: tiles[k] for k, pair in enumerate(pairs)}

    start_weights = jnp.concatenate([coefficients, velocity], axis=1)
    every_weights = gather_by_permutes(start_weights, "path").transpose(1, 0, 2)
    every_weights = every_weights.reshape(start_weights.shape[0], n_path * 2 * paths)
    partial = kernel_apply(all_rows, square_norms(all_rows), records, work_norms, every_weights)
    partial = partial.reshape(n_blk, steps * share, n_path, 2 * paths).transpose(0, 2, 1, 3)
    got = lax.all_to_all(
        partial.reshape(n_blk * n_path, -1), ("blk", "path"), 0, 0, tiled=True
    )
    got = jnp.sum(got.reshape(n_blk, n_path, steps, share, 2 * paths), axis=0)
    start_sums = got.transpose(1, 0, 2, 3).reshape(steps, slot_count, 2 * paths)

    a_weight, b_weight = velocity_weights(steps + 1)
    own_rows_norms = square_norms(own_rows)
    cand_norms = square_norms(candidates)
    neighbour_norms = square_norms(neighbour)
    own_start = kernel_apply(candidates, cand_norms, records, work_norms, start_weights)
    next_start = kernel_apply(neighbour, neighbour_norms, records, work_norms, start_weights)
    own_slots = kernel_tile_of(candidates, cand_norms, own_rows, own_rows_norms)
    next_slots = kernel_tile_of(neighbour, neighbour_norms, own_rows, own_rows_norms)
    weighted_updates = []
    updates = []
    for repeat in range(steps):
        local_rows = block_local[repeat]
        own_count = lax.dynamic_index_in_dim(block_count[repeat], own_index, 0, keepdims=False)
        is_live = slot_ids < own_count
        total = start_sums[repeat, :, :paths]
        if repeat > 0:
            total = total + a_weight[repeat] * start_sums[repeat, :, paths:]
        for earlier in range(repeat):
            cross = jnp.dot(
                tile_of[(repeat, earlier)], updates[earlier], precision=lax.Precision.HIGH
            )
            total = total + b_weight[repeat][earlier] * cross
        product = total / root_count
        gradient = jnp.where(
            is_live[:, None], product + NOISE * coefficients[local_rows] - targets[local_rows], 0.0
        )
        step_update = -RATE * gradient
        velocity = (MOMENTUM * velocity).at[local_rows].add(step_update)
        coefficients = coefficients + velocity
        weighted_updates.append(b_weight[steps][repeat] * step_update)
        if repeat < steps - 1:
            updates.append(gather_blocks(step_update, "blk").reshape(n_blk * slot_count, paths))

    slot_weights = jnp.concatenate(weighted_updates, axis=0)
    own_sum = (
        own_start[:, :paths]
        + a_weight[steps] * own_start[:, paths:]
        + jnp.dot(own_slots, slot_weights, precision=lax.Precision.HIGH)
    )
    next_sum = (
        next_start[:, :paths]
        + a_weight[steps] * next_start[:, paths:]
        + jnp.dot(next_slots, slot_weights, precision=lax.Precision.HIGH)
    )
    first_part = prior + own_sum / root_count
    next_term = next_sum / root_count
    scores = passed_along(first_part, "blk", 2) + passed_along(next_term, "blk", 1)
    squares_local = jnp.sum(scores * scores, axis=1)
    summed = lax.psum(squares_local, "path")
    path_rms = jnp.sqrt(summed / (scores.shape[1] * lax.axis_size("path")) + EPSILON)
    return (coefficients, velocity, scores, path_rms)


def solution(mesh):
    return jax.shard_map(
        shards,
        mesh=mesh,
        in_specs=(
            P("blk", None),
            P("blk", "path"),
            P("blk", "path"),
            P("blk", "path"),
            P(None, "blk"),
            P(),
            P("blk", None),
            P(),
            P(),
            P(None, "path"),
        ),
        out_specs=(P("blk", "path"), P("blk", "path"), P("blk", "path"), P("blk")),
        check_vma=False,
    )
```

```python
import math

import jax
import jax.numpy as jnp
from jax import lax
from jax.sharding import PartitionSpec as P

NOISE = 0.5
MOMENTUM = 0.9
RATE = 0.3
EPSILON = 1e-06
SIGNAL = 9.0


def passed_along(shard, axis, by):
    length = lax.axis_size(axis)
    return lax.ppermute(shard, axis, [(i, (i + by) % length) for i in range(length)])


def square_norms(row_block):
    widened = row_block.astype(jnp.float32)
    return jnp.sum(widened * widened, axis=1)


def kernel_tile_of(left_rows, left_norms, right_rows, right_norms):
    dot_values = lax.dot_general(
        left_rows, right_rows, (((1,), (1,)), ((), ())), preferred_element_type=jnp.float32
    )
    distance = left_norms[:, None] + right_norms[None, :] - 2.0 * dot_values
    return SIGNAL * jnp.exp(-distance / left_rows.shape[1])


def kernel_apply(left_rows, left_norms, right_rows, right_norms, weights):
    kernel_tile = kernel_tile_of(left_rows, left_norms, right_rows, right_norms)
    return jnp.dot(kernel_tile, weights, precision=lax.Precision.HIGH)


def prior_values(cand_rows, frequencies, phases, prior_weight):
    angles = (
        jnp.dot(cand_rows, frequencies, preferred_element_type=jnp.float32) * math.sqrt(2.0)
        + phases[None, :]
    )
    features = math.sqrt(2.0 * SIGNAL / frequencies.shape[1]) * jnp.cos(angles)
    return jnp.dot(features, prior_weight, precision=lax.Precision.HIGHEST)


def gather_blocks(block, axis):
    length = lax.axis_size(axis)
    flat = block.reshape(1, -1)
    spread = jnp.broadcast_to(flat, (length, flat.shape[1]))
    got = lax.all_to_all(spread, axis, 0, 0, tiled=True)
    return got.reshape((length,) + block.shape)


def gather_stack(block, axis):
    length = lax.axis_size(axis)
    spread = jnp.broadcast_to(block[None], (length,) + block.shape)
    return lax.all_to_all(spread, axis, 0, 0, tiled=True)


def gather_by_permutes(block, axis):
    length = lax.axis_size(axis)
    here = lax.axis_index(axis)
    moved = [block] + [passed_along(block, axis, by) for by in range(1, length)]
    order = (here - jnp.arange(length, dtype=jnp.int32)) % length
    return jnp.take(jnp.stack(moved), order, axis=0)


def sum_to_owners(partial, axis):
    length = lax.axis_size(axis)
    flat = partial.reshape(length, -1)
    got = lax.all_to_all(flat, axis, 0, 0, tiled=True)
    return jnp.sum(got, axis=0).reshape(partial.shape[1:])


def velocity_weights(steps):
    a, b = [], []
    for t in range(steps):
        a.append(sum(MOMENTUM ** u for u in range(1, t + 1)))
        b.append([sum(MOMENTUM ** (u - 1 - s) for u in range(s + 1, t + 1)) for s in range(t)])
    return a, b


def shards(
    records,
    coefficients,
    velocity,
    targets,
    block_local,
    block_count,
    candidates,
    frequencies,
    phases,
    prior_weight,
):
    n_blk = lax.axis_size("blk")
    record_total = records.shape[0] * n_blk
    root_count = jnp.sqrt(jnp.float32(record_total))
    steps, slot_count = block_local.shape
    own_index = lax.axis_index("blk")
    neighbour = passed_along(candidates, "blk", 1)
    work_norms = square_norms(records)
    slot_ids = jnp.arange(slot_count, dtype=jnp.int32)
    paths = coefficients.shape[1]

    n_path = lax.axis_size("path")
    path_index = lax.axis_index("path")
    share = slot_count // n_path
    own_rows = records[block_local.reshape(-1)]

    share_local = lax.dynamic_slice_in_dim(block_local, path_index * share, share, axis=1)
    share_rows = records[share_local.reshape(-1)]
    gathered = gather_stack(share_rows, "blk")
    all_rows = gathered.reshape(n_blk * steps * share, -1)
    start_weights = jnp.concatenate([coefficients, velocity], axis=1)
    every_weights = gather_by_permutes(start_weights, "path").transpose(1, 0, 2)
    every_weights = every_weights.reshape(start_weights.shape[0], n_path * 2 * paths)
    partial = kernel_apply(all_rows, square_norms(all_rows), records, work_norms, every_weights)
    partial, candidates, neighbour = lax.optimization_barrier((partial, candidates, neighbour))
    share_sums = sum_to_owners(partial.reshape(n_blk, steps * share, n_path * 2 * paths), "blk")
    share_sums = share_sums.reshape(steps * share, n_path, 2 * paths).transpose(1, 0, 2)
    got = lax.all_to_all(share_sums, "path", 0, 0, tiled=True)
    start_sums = got.reshape(n_path, steps, share, 2 * paths).transpose(1, 0, 2, 3)
    start_sums = start_sums.reshape(steps, slot_count, 2 * paths)

    pairs = [(t, s) for t in range(steps) for s in range(t)]
    tiles = []
    for t, s in pairs:
        mine = own_rows[t * slot_count:(t + 1) * slot_count]
        theirs = gathered[:, s * share:(s + 1) * share].reshape(n_blk * share, -1)
        tiles.append(kernel_tile_of(mine, square_norms(mine), theirs, square_norms(theirs)))
    tiles = gather_by_permutes(jnp.stack(tiles), "path")
    tiles = tiles.reshape(n_path, len(pairs), slot_count, n_blk, share).transpose(1, 2, 3, 0, 4)
    tiles = tiles.reshape(len(pairs), slot_count, n_blk * slot_count)
    tile_of = {pair: tiles[k] for k, pair in enumerate(pairs)}

    a_weight, b_weight = velocity_weights(steps + 1)
    prior = prior_values(candidates, frequencies, phases, prior_weight)
    own_rows_norms = square_norms(own_rows)
    cand_norms = square_norms(candidates)
    neighbour_norms = square_norms(neighbour)
    own_start = kernel_apply(candidates, cand_norms, records, work_norms, start_weights)
    next_start = kernel_apply(neighbour, neighbour_norms, records, work_norms, start_weights)
    own_slots = kernel_tile_of(candidates, cand_norms, own_rows, own_rows_norms)
    next_slots = kernel_tile_of(neighbour, neighbour_norms, own_rows, own_rows_norms)
    weighted_updates = []
    updates = []
    for repeat in range(steps):
        local_rows = block_local[repeat]
        own_count = lax.dynamic_index_in_dim(block_count[repeat], own_index, 0, keepdims=False)
        is_live = slot_ids < own_count
        total = start_sums[repeat, :, :paths]
        if repeat > 0:
            total = total + a_weight[repeat] * start_sums[repeat, :, paths:]
        for earlier in range(repeat):
            cross = jnp.dot(
                tile_of[(repeat, earlier)], updates[earlier], precision=lax.Precision.HIGH
            )
            total = total + b_weight[repeat][earlier] * cross
        product = total / root_count
        gradient = jnp.where(
            is_live[:, None], product + NOISE * coefficients[local_rows] - targets[local_rows], 0.0
        )
        step_update = -RATE * gradient
        velocity = (MOMENTUM * velocity).at[local_rows].add(step_update)
        coefficients = coefficients + velocity
        weighted_updates.append(b_weight[steps][repeat] * step_update)
        if repeat < steps - 1:
            updates.append(gather_blocks(step_update, "blk").reshape(n_blk * slot_count, paths))

    slot_weights = jnp.concatenate(weighted_updates, axis=0)
    own_sum = (
        own_start[:, :paths]
        + a_weight[steps] * own_start[:, paths:]
        + jnp.dot(own_slots, slot_weights, precision=lax.Precision.HIGH)
    )
    next_sum = (
        next_start[:, :paths]
        + a_weight[steps] * next_start[:, paths:]
        + jnp.dot(next_slots, slot_weights, precision=lax.Precision.HIGH)
    )
    first_part = prior + own_sum / root_count
    next_term = next_sum / root_count
    scores = passed_along(first_part, "blk", 2) + passed_along(next_term, "blk", 1)
    squares_local = jnp.sum(scores * scores, axis=1)
    summed = lax.psum(squares_local, "path")
    path_rms = jnp.sqrt(summed / (scores.shape[1] * lax.axis_size("path")) + EPSILON)
    return (coefficients, velocity, scores, path_rms)


def solution(mesh):
    return jax.shard_map(
        shards,
        mesh=mesh,
        in_specs=(
            P("blk", None),
            P("blk", "path"),
            P("blk", "path"),
            P("blk", "path"),
            P(None, "blk"),
            P(),
            P("blk", None),
            P(),
            P(),
            P(None, "path"),
        ),
        out_specs=(P("blk", "path"), P("blk", "path"), P("blk", "path"), P("blk")),
        check_vma=False,
    )
```

```python
import math

import jax
import jax.numpy as jnp
from jax import lax
from jax.sharding import PartitionSpec as P

NOISE = 0.5
MOMENTUM = 0.9
RATE = 0.3
EPSILON = 1e-06
SIGNAL = 9.0


def passed_along(shard, axis, by):
    length = lax.axis_size(axis)
    return lax.ppermute(shard, axis, [(i, (i + by) % length) for i in range(length)])


def square_norms(row_block):
    widened = row_block.astype(jnp.float32)
    return jnp.sum(widened * widened, axis=1)


def kernel_tile_of(left_rows, left_norms, right_rows, right_norms):
    dot_values = lax.dot_general(
        left_rows, right_rows, (((1,), (1,)), ((), ())), preferred_element_type=jnp.float32
    )
    distance = left_norms[:, None] + right_norms[None, :] - 2.0 * dot_values
    return SIGNAL * jnp.exp(-distance / left_rows.shape[1])


def kernel_apply(left_rows, left_norms, right_rows, right_norms, weights):
    kernel_tile = kernel_tile_of(left_rows, left_norms, right_rows, right_norms)
    return jnp.dot(kernel_tile, weights, precision=lax.Precision.HIGH)


def prior_values(cand_rows, frequencies, phases, prior_weight):
    angles = (
        jnp.dot(cand_rows, frequencies, preferred_element_type=jnp.float32) * math.sqrt(2.0)
        + phases[None, :]
    )
    features = math.sqrt(2.0 * SIGNAL / frequencies.shape[1]) * jnp.cos(angles)
    return jnp.dot(features, prior_weight, precision=lax.Precision.HIGHEST)


def gather_blocks(block, axis):
    length = lax.axis_size(axis)
    flat = block.reshape(1, -1)
    spread = jnp.broadcast_to(flat, (length, flat.shape[1]))
    got = lax.all_to_all(spread, axis, 0, 0, tiled=True)
    return got.reshape((length,) + block.shape)


def gather_stack(block, axis):
    length = lax.axis_size(axis)
    spread = jnp.broadcast_to(block[None], (length,) + block.shape)
    return lax.all_to_all(spread, axis, 0, 0, tiled=True)


def gather_by_permutes(block, axis):
    length = lax.axis_size(axis)
    here = lax.axis_index(axis)
    moved = [block] + [passed_along(block, axis, by) for by in range(1, length)]
    order = (here - jnp.arange(length, dtype=jnp.int32)) % length
    return jnp.take(jnp.stack(moved), order, axis=0)


def sum_to_owners(partial, axis):
    length = lax.axis_size(axis)
    flat = partial.reshape(length, -1)
    got = lax.all_to_all(flat, axis, 0, 0, tiled=True)
    return jnp.sum(got, axis=0).reshape(partial.shape[1:])


def velocity_weights(steps):
    a, b = [], []
    for t in range(steps):
        a.append(sum(MOMENTUM ** u for u in range(1, t + 1)))
        b.append([sum(MOMENTUM ** (u - 1 - s) for u in range(s + 1, t + 1)) for s in range(t)])
    return a, b


def shards(
    records,
    coefficients,
    velocity,
    targets,
    block_local,
    block_count,
    candidates,
    frequencies,
    phases,
    prior_weight,
):
    n_blk = lax.axis_size("blk")
    record_total = records.shape[0] * n_blk
    root_count = jnp.sqrt(jnp.float32(record_total))
    steps, slot_count = block_local.shape
    own_index = lax.axis_index("blk")
    neighbour = passed_along(candidates, "blk", 1)
    work_norms = square_norms(records)
    slot_ids = jnp.arange(slot_count, dtype=jnp.int32)
    paths = coefficients.shape[1]

    n_path = lax.axis_size("path")
    path_index = lax.axis_index("path")
    share = slot_count // n_path
    own_rows = records[block_local.reshape(-1)]
    prior = prior_values(candidates, frequencies, phases, prior_weight)

    share_local = lax.dynamic_slice_in_dim(block_local, path_index * share, share, axis=1)
    share_rows = records[share_local.reshape(-1)]
    gathered = gather_stack(share_rows, "blk")
    gathered, prior = lax.optimization_barrier((gathered, prior))
    all_rows = gathered.reshape(n_blk * steps * share, -1)
    start_weights = jnp.concatenate([coefficients, velocity], axis=1)
    every_weights = gather_by_permutes(start_weights, "path").transpose(1, 0, 2)
    every_weights = every_weights.reshape(start_weights.shape[0], n_path * 2 * paths)
    partial = kernel_apply(all_rows, square_norms(all_rows), records, work_norms, every_weights)
    partial = partial.reshape(n_blk, steps * share, n_path, 2 * paths).transpose(0, 2, 1, 3)
    got = lax.all_to_all(
        partial.reshape(n_blk * n_path, -1), ("blk", "path"), 0, 0, tiled=True
    )
    got = jnp.sum(got.reshape(n_blk, n_path, steps, share, 2 * paths), axis=0)
    start_sums = got.transpose(1, 0, 2, 3).reshape(steps, slot_count, 2 * paths)

    pairs = [(t, s) for t in range(steps) for s in range(t)]
    tiles = []
    for t, s in pairs:
        mine = own_rows[t * slot_count:(t + 1) * slot_count]
        theirs = gathered[:, s * share:(s + 1) * share].reshape(n_blk * share, -1)
        tiles.append(kernel_tile_of(mine, square_norms(mine), theirs, square_norms(theirs)))
    tiles = gather_by_permutes(jnp.stack(tiles), "path")
    tiles = tiles.reshape(n_path, len(pairs), slot_count, n_blk, share).transpose(1, 2, 3, 0, 4)
    tiles = tiles.reshape(len(pairs), slot_count, n_blk * slot_count)
    tile_of = {pair: tiles[k] for k, pair in enumerate(pairs)}

    a_weight, b_weight = velocity_weights(steps + 1)
    own_rows_norms = square_norms(own_rows)
    cand_norms = square_norms(candidates)
    neighbour_norms = square_norms(neighbour)
    own_start = kernel_apply(candidates, cand_norms, records, work_norms, start_weights)
    next_start = kernel_apply(neighbour, neighbour_norms, records, work_norms, start_weights)
    own_slots = kernel_tile_of(candidates, cand_norms, own_rows, own_rows_norms)
    next_slots = kernel_tile_of(neighbour, neighbour_norms, own_rows, own_rows_norms)
    weighted_updates = []
    updates = []
    for repeat in range(steps):
        local_rows = block_local[repeat]
        own_count = lax.dynamic_index_in_dim(block_count[repeat], own_index, 0, keepdims=False)
        is_live = slot_ids < own_count
        total = start_sums[repeat, :, :paths]
        if repeat > 0:
            total = total + a_weight[repeat] * start_sums[repeat, :, paths:]
        for earlier in range(repeat):
            cross = jnp.dot(
                tile_of[(repeat, earlier)], updates[earlier], precision=lax.Precision.HIGH
            )
            total = total + b_weight[repeat][earlier] * cross
        product = total / root_count
        gradient = jnp.where(
            is_live[:, None], product + NOISE * coefficients[local_rows] - targets[local_rows], 0.0
        )
        step_update = -RATE * gradient
        velocity = (MOMENTUM * velocity).at[local_rows].add(step_update)
        coefficients = coefficients + velocity
        weighted_updates.append(b_weight[steps][repeat] * step_update)
        if repeat < steps - 1:
            updates.append(gather_blocks(step_update, "blk").reshape(n_blk * slot_count, paths))

    slot_weights = jnp.concatenate(weighted_updates, axis=0)
    own_sum = (
        own_start[:, :paths]
        + a_weight[steps] * own_start[:, paths:]
        + jnp.dot(own_slots, slot_weights, precision=lax.Precision.HIGH)
    )
    next_sum = (
        next_start[:, :paths]
        + a_weight[steps] * next_start[:, paths:]
        + jnp.dot(next_slots, slot_weights, precision=lax.Precision.HIGH)
    )
    first_part = prior + own_sum / root_count
    next_term = next_sum / root_count
    scores = passed_along(first_part, "blk", 2) + passed_along(next_term, "blk", 1)
    squares_local = jnp.sum(scores * scores, axis=1)
    summed = lax.psum(squares_local, "path")
    path_rms = jnp.sqrt(summed / (scores.shape[1] * lax.axis_size("path")) + EPSILON)
    return (coefficients, velocity, scores, path_rms)


def solution(mesh):
    return jax.shard_map(
        shards,
        mesh=mesh,
        in_specs=(
            P("blk", None),
            P("blk", "path"),
            P("blk", "path"),
            P("blk", "path"),
            P(None, "blk"),
            P(),
            P("blk", None),
            P(),
            P(),
            P(None, "path"),
        ),
        out_specs=(P("blk", "path"), P("blk", "path"), P("blk", "path"), P("blk")),
        check_vma=False,
    )
```

```python
import math

import jax
import jax.numpy as jnp
from jax import lax
from jax.sharding import PartitionSpec as P

NOISE = 0.5
MOMENTUM = 0.9
RATE = 0.3
EPSILON = 1e-06
SIGNAL = 9.0


def passed_along(shard, axis, by):
    length = lax.axis_size(axis)
    return lax.ppermute(shard, axis, [(i, (i + by) % length) for i in range(length)])


def square_norms(row_block):
    widened = row_block.astype(jnp.float32)
    return jnp.sum(widened * widened, axis=1)


def kernel_tile_of(left_rows, left_norms, right_rows, right_norms):
    dot_values = lax.dot_general(
        left_rows, right_rows, (((1,), (1,)), ((), ())), preferred_element_type=jnp.float32
    )
    distance = left_norms[:, None] + right_norms[None, :] - 2.0 * dot_values
    return SIGNAL * jnp.exp(-distance / left_rows.shape[1])


def kernel_apply(left_rows, left_norms, right_rows, right_norms, weights):
    kernel_tile = kernel_tile_of(left_rows, left_norms, right_rows, right_norms)
    return jnp.dot(kernel_tile, weights, precision=lax.Precision.HIGH)


def prior_values(cand_rows, frequencies, phases, prior_weight):
    angles = (
        jnp.dot(cand_rows, frequencies, preferred_element_type=jnp.float32) * math.sqrt(2.0)
        + phases[None, :]
    )
    features = math.sqrt(2.0 * SIGNAL / frequencies.shape[1]) * jnp.cos(angles)
    return jnp.dot(features, prior_weight, precision=lax.Precision.HIGHEST)


def gather_blocks(block, axis):
    length = lax.axis_size(axis)
    flat = block.reshape(1, -1)
    spread = jnp.broadcast_to(flat, (length, flat.shape[1]))
    got = lax.all_to_all(spread, axis, 0, 0, tiled=True)
    return got.reshape((length,) + block.shape)


def gather_stack(block, axis):
    length = lax.axis_size(axis)
    spread = jnp.broadcast_to(block[None], (length,) + block.shape)
    return lax.all_to_all(spread, axis, 0, 0, tiled=True)


def gather_by_permutes(block, axis):
    length = lax.axis_size(axis)
    here = lax.axis_index(axis)
    moved = [block] + [passed_along(block, axis, by) for by in range(1, length)]
    order = (here - jnp.arange(length, dtype=jnp.int32)) % length
    return jnp.take(jnp.stack(moved), order, axis=0)


def sum_to_owners(partial, axis):
    length = lax.axis_size(axis)
    flat = partial.reshape(length, -1)
    got = lax.all_to_all(flat, axis, 0, 0, tiled=True)
    return jnp.sum(got, axis=0).reshape(partial.shape[1:])


def velocity_weights(steps):
    a, b = [], []
    for t in range(steps):
        a.append(sum(MOMENTUM ** u for u in range(1, t + 1)))
        b.append([sum(MOMENTUM ** (u - 1 - s) for u in range(s + 1, t + 1)) for s in range(t)])
    return a, b


def shards(
    records,
    coefficients,
    velocity,
    targets,
    block_local,
    block_count,
    candidates,
    frequencies,
    phases,
    prior_weight,
):
    n_blk = lax.axis_size("blk")
    record_total = records.shape[0] * n_blk
    root_count = jnp.sqrt(jnp.float32(record_total))
    steps, slot_count = block_local.shape
    own_index = lax.axis_index("blk")
    work_norms = square_norms(records)
    slot_ids = jnp.arange(slot_count, dtype=jnp.int32)
    paths = coefficients.shape[1]

    n_path = lax.axis_size("path")
    path_index = lax.axis_index("path")
    share = slot_count // n_path
    own_rows = records[block_local.reshape(-1)]
    prior = prior_values(candidates, frequencies, phases, prior_weight)

    share_local = lax.dynamic_slice_in_dim(block_local, path_index * share, share, axis=1)
    share_rows = records[share_local.reshape(-1)]
    gathered = gather_stack(share_rows, "blk")
    gathered, prior = lax.optimization_barrier((gathered, prior))
    all_rows = gathered.reshape(n_blk * steps * share, -1)
    start_weights = jnp.concatenate([coefficients, velocity], axis=1)
    every_weights = gather_by_permutes(start_weights, "path").transpose(1, 0, 2)
    every_weights = every_weights.reshape(start_weights.shape[0], n_path * 2 * paths)
    partial = kernel_apply(all_rows, square_norms(all_rows), records, work_norms, every_weights)
    partial, late_candidates = lax.optimization_barrier((partial, candidates))
    neighbour = passed_along(late_candidates, "blk", 1)
    share_sums = sum_to_owners(partial.reshape(n_blk, steps * share, n_path * 2 * paths), "blk")
    share_sums = share_sums.reshape(steps * share, n_path, 2 * paths).transpose(1, 0, 2)
    got = lax.all_to_all(share_sums, "path", 0, 0, tiled=True)
    start_sums = got.reshape(n_path, steps, share, 2 * paths).transpose(1, 0, 2, 3)
    start_sums = start_sums.reshape(steps, slot_count, 2 * paths)

    pairs = [(t, s) for t in range(steps) for s in range(t)]
    tiles = []
    for t, s in pairs:
        mine = own_rows[t * slot_count:(t + 1) * slot_count]
        theirs = gathered[:, s * share:(s + 1) * share].reshape(n_blk * share, -1)
        tiles.append(kernel_tile_of(mine, square_norms(mine), theirs, square_norms(theirs)))
    tiles = gather_by_permutes(jnp.stack(tiles), "path")
    tiles = tiles.reshape(n_path, len(pairs), slot_count, n_blk, share).transpose(1, 2, 3, 0, 4)
    tiles = tiles.reshape(len(pairs), slot_count, n_blk * slot_count)
    tile_of = {pair: tiles[k] for k, pair in enumerate(pairs)}

    a_weight, b_weight = velocity_weights(steps + 1)
    own_rows_norms = square_norms(own_rows)
    cand_norms = square_norms(candidates)
    neighbour_norms = square_norms(neighbour)
    own_start = kernel_apply(candidates, cand_norms, records, work_norms, start_weights)
    next_start = kernel_apply(neighbour, neighbour_norms, records, work_norms, start_weights)
    own_slots = kernel_tile_of(candidates, cand_norms, own_rows, own_rows_norms)
    next_slots = kernel_tile_of(neighbour, neighbour_norms, own_rows, own_rows_norms)
    weighted_updates = []
    updates = []
    for repeat in range(steps):
        local_rows = block_local[repeat]
        own_count = lax.dynamic_index_in_dim(block_count[repeat], own_index, 0, keepdims=False)
        is_live = slot_ids < own_count
        total = start_sums[repeat, :, :paths]
        if repeat > 0:
            total = total + a_weight[repeat] * start_sums[repeat, :, paths:]
        for earlier in range(repeat):
            cross = jnp.dot(
                tile_of[(repeat, earlier)], updates[earlier], precision=lax.Precision.HIGH
            )
            total = total + b_weight[repeat][earlier] * cross
        product = total / root_count
        gradient = jnp.where(
            is_live[:, None], product + NOISE * coefficients[local_rows] - targets[local_rows], 0.0
        )
        step_update = -RATE * gradient
        velocity = (MOMENTUM * velocity).at[local_rows].add(step_update)
        coefficients = coefficients + velocity
        weighted_updates.append(b_weight[steps][repeat] * step_update)
        if repeat < steps - 1:
            updates.append(gather_blocks(step_update, "blk").reshape(n_blk * slot_count, paths))

    slot_weights = jnp.concatenate(weighted_updates, axis=0)
    own_sum = (
        own_start[:, :paths]
        + a_weight[steps] * own_start[:, paths:]
        + jnp.dot(own_slots, slot_weights, precision=lax.Precision.HIGH)
    )
    next_sum = (
        next_start[:, :paths]
        + a_weight[steps] * next_start[:, paths:]
        + jnp.dot(next_slots, slot_weights, precision=lax.Precision.HIGH)
    )
    first_part = prior + own_sum / root_count
    next_term = next_sum / root_count
    scores = passed_along(first_part, "blk", 2) + passed_along(next_term, "blk", 1)
    squares_local = jnp.sum(scores * scores, axis=1)
    summed = lax.psum(squares_local, "path")
    path_rms = jnp.sqrt(summed / (scores.shape[1] * lax.axis_size("path")) + EPSILON)
    return (coefficients, velocity, scores, path_rms)


def solution(mesh):
    return jax.shard_map(
        shards,
        mesh=mesh,
        in_specs=(
            P("blk", None),
            P("blk", "path"),
            P("blk", "path"),
            P("blk", "path"),
            P(None, "blk"),
            P(),
            P("blk", None),
            P(),
            P(),
            P(None, "path"),
        ),
        out_specs=(P("blk", "path"), P("blk", "path"), P("blk", "path"), P("blk")),
        check_vma=False,
    )
```

```python
import math

import jax
import jax.numpy as jnp
from jax import lax
from jax.sharding import PartitionSpec as P

NOISE = 0.5
MOMENTUM = 0.9
RATE = 0.3
EPSILON = 1e-06
SIGNAL = 9.0


def passed_along(shard, axis, by):
    length = lax.axis_size(axis)
    return lax.ppermute(shard, axis, [(i, (i + by) % length) for i in range(length)])


def square_norms(row_block):
    widened = row_block.astype(jnp.float32)
    return jnp.sum(widened * widened, axis=1)


def kernel_tile_of(left_rows, left_norms, right_rows, right_norms):
    dot_values = lax.dot_general(
        left_rows, right_rows, (((1,), (1,)), ((), ())), preferred_element_type=jnp.float32
    )
    distance = left_norms[:, None] + right_norms[None, :] - 2.0 * dot_values
    return SIGNAL * jnp.exp(-distance / left_rows.shape[1])


def kernel_apply(left_rows, left_norms, right_rows, right_norms, weights):
    kernel_tile = kernel_tile_of(left_rows, left_norms, right_rows, right_norms)
    return jnp.dot(kernel_tile, weights, precision=lax.Precision.HIGH)


def prior_values(cand_rows, frequencies, phases, prior_weight):
    angles = (
        jnp.dot(cand_rows, frequencies, preferred_element_type=jnp.float32) * math.sqrt(2.0)
        + phases[None, :]
    )
    features = math.sqrt(2.0 * SIGNAL / frequencies.shape[1]) * jnp.cos(angles)
    return jnp.dot(features, prior_weight, precision=lax.Precision.HIGHEST)


def gather_blocks(block, axis):
    length = lax.axis_size(axis)
    flat = block.reshape(1, -1)
    spread = jnp.broadcast_to(flat, (length, flat.shape[1]))
    got = lax.all_to_all(spread, axis, 0, 0, tiled=True)
    return got.reshape((length,) + block.shape)


def gather_stack(block, axis):
    length = lax.axis_size(axis)
    spread = jnp.broadcast_to(block[None], (length,) + block.shape)
    return lax.all_to_all(spread, axis, 0, 0, tiled=True)


def gather_by_permutes(block, axis):
    length = lax.axis_size(axis)
    here = lax.axis_index(axis)
    moved = [block] + [passed_along(block, axis, by) for by in range(1, length)]
    order = (here - jnp.arange(length, dtype=jnp.int32)) % length
    return jnp.take(jnp.stack(moved), order, axis=0)


def sum_to_owners(partial, axis):
    length = lax.axis_size(axis)
    flat = partial.reshape(length, -1)
    got = lax.all_to_all(flat, axis, 0, 0, tiled=True)
    return jnp.sum(got, axis=0).reshape(partial.shape[1:])


def velocity_weights(steps):
    a, b = [], []
    for t in range(steps):
        a.append(sum(MOMENTUM ** u for u in range(1, t + 1)))
        b.append([sum(MOMENTUM ** (u - 1 - s) for u in range(s + 1, t + 1)) for s in range(t)])
    return a, b


def shards(
    records,
    coefficients,
    velocity,
    targets,
    block_local,
    block_count,
    candidates,
    frequencies,
    phases,
    prior_weight,
):
    n_blk = lax.axis_size("blk")
    record_total = records.shape[0] * n_blk
    root_count = jnp.sqrt(jnp.float32(record_total))
    steps, slot_count = block_local.shape
    own_index = lax.axis_index("blk")
    work_norms = square_norms(records)
    slot_ids = jnp.arange(slot_count, dtype=jnp.int32)
    paths = coefficients.shape[1]

    n_path = lax.axis_size("path")
    path_index = lax.axis_index("path")
    share = slot_count // n_path
    own_rows = records[block_local.reshape(-1)]
    prior = prior_values(candidates, frequencies, phases, prior_weight)

    share_local = lax.dynamic_slice_in_dim(block_local, path_index * share, share, axis=1)
    share_rows = records[share_local.reshape(-1)]
    gathered = gather_stack(share_rows, "blk")
    gathered, prior = lax.optimization_barrier((gathered, prior))
    all_rows = gathered.reshape(n_blk * steps * share, -1)
    start_weights = jnp.concatenate([coefficients, velocity], axis=1)
    every_weights = gather_by_permutes(start_weights, "path").transpose(1, 0, 2)
    every_weights = every_weights.reshape(start_weights.shape[0], n_path * 2 * paths)
    partial = kernel_apply(all_rows, square_norms(all_rows), records, work_norms, every_weights)
    partial, late_candidates = lax.optimization_barrier((partial, candidates))
    neighbour = passed_along(late_candidates, "blk", 1)
    share_sums = sum_to_owners(partial.reshape(n_blk, steps * share, n_path * 2 * paths), "blk")
    share_sums = share_sums.reshape(steps * share, n_path, 2 * paths).transpose(1, 0, 2)
    got = lax.all_to_all(share_sums, "path", 0, 0, tiled=True)
    start_sums = got.reshape(n_path, steps, share, 2 * paths).transpose(1, 0, 2, 3)
    start_sums = start_sums.reshape(steps, slot_count, 2 * paths)

    pairs = [(t, s) for t in range(steps) for s in range(t)]
    tiles = []
    for t, s in pairs:
        mine = own_rows[t * slot_count:(t + 1) * slot_count]
        theirs = gathered[:, s * share:(s + 1) * share].reshape(n_blk * share, -1)
        tiles.append(kernel_tile_of(mine, square_norms(mine), theirs, square_norms(theirs)))
    tiles = gather_by_permutes(jnp.stack(tiles), "path")
    tiles = tiles.reshape(n_path, len(pairs), slot_count, n_blk, share).transpose(1, 2, 3, 0, 4)
    tiles = tiles.reshape(len(pairs), slot_count, n_blk * slot_count)
    tile_of = {pair: tiles[k] for k, pair in enumerate(pairs)}

    a_weight, b_weight = velocity_weights(steps + 1)
    own_rows_norms = square_norms(own_rows)
    cand_norms = square_norms(candidates)
    own_start = kernel_apply(candidates, cand_norms, records, work_norms, start_weights)
    own_slots = kernel_tile_of(candidates, cand_norms, own_rows, own_rows_norms)
    weighted_updates = []
    updates = []
    for repeat in range(steps):
        local_rows = block_local[repeat]
        own_count = lax.dynamic_index_in_dim(block_count[repeat], own_index, 0, keepdims=False)
        is_live = slot_ids < own_count
        total = start_sums[repeat, :, :paths]
        if repeat > 0:
            total = total + a_weight[repeat] * start_sums[repeat, :, paths:]
        for earlier in range(repeat):
            cross = jnp.dot(
                tile_of[(repeat, earlier)], updates[earlier], precision=lax.Precision.HIGH
            )
            total = total + b_weight[repeat][earlier] * cross
        product = total / root_count
        gradient = jnp.where(
            is_live[:, None], product + NOISE * coefficients[local_rows] - targets[local_rows], 0.0
        )
        step_update = -RATE * gradient
        velocity = (MOMENTUM * velocity).at[local_rows].add(step_update)
        coefficients = coefficients + velocity
        weighted_updates.append(b_weight[steps][repeat] * step_update)
        if repeat == steps - 2:
            last_exchanged = step_update
        if repeat < steps - 1:
            updates.append(gather_blocks(step_update, "blk").reshape(n_blk * slot_count, paths))

    neighbour, _ = lax.optimization_barrier((neighbour, last_exchanged))
    neighbour_norms = square_norms(neighbour)
    next_start = kernel_apply(neighbour, neighbour_norms, records, work_norms, start_weights)
    next_slots = kernel_tile_of(neighbour, neighbour_norms, own_rows, own_rows_norms)

    slot_weights = jnp.concatenate(weighted_updates, axis=0)
    own_sum = (
        own_start[:, :paths]
        + a_weight[steps] * own_start[:, paths:]
        + jnp.dot(own_slots, slot_weights, precision=lax.Precision.HIGH)
    )
    next_sum = (
        next_start[:, :paths]
        + a_weight[steps] * next_start[:, paths:]
        + jnp.dot(next_slots, slot_weights, precision=lax.Precision.HIGH)
    )
    first_part = prior + own_sum / root_count
    next_term = next_sum / root_count
    scores = passed_along(first_part, "blk", 2) + passed_along(next_term, "blk", 1)
    squares_local = jnp.sum(scores * scores, axis=1)
    summed = lax.psum(squares_local, "path")
    path_rms = jnp.sqrt(summed / (scores.shape[1] * lax.axis_size("path")) + EPSILON)
    return (coefficients, velocity, scores, path_rms)


def solution(mesh):
    return jax.shard_map(
        shards,
        mesh=mesh,
        in_specs=(
            P("blk", None),
            P("blk", "path"),
            P("blk", "path"),
            P("blk", "path"),
            P(None, "blk"),
            P(),
            P("blk", None),
            P(),
            P(),
            P(None, "path"),
        ),
        out_specs=(P("blk", "path"), P("blk", "path"), P("blk", "path"), P("blk")),
        check_vma=False,
    )
```

```python
import math

import jax
import jax.numpy as jnp
from jax import lax
from jax.sharding import PartitionSpec as P

NOISE = 0.5
MOMENTUM = 0.9
RATE = 0.3
EPSILON = 1e-06
SIGNAL = 9.0


def passed_along(shard, axis, by):
    length = lax.axis_size(axis)
    return lax.ppermute(shard, axis, [(i, (i + by) % length) for i in range(length)])


def square_norms(row_block):
    widened = row_block.astype(jnp.float32)
    return jnp.sum(widened * widened, axis=1)


def kernel_tile_of(left_rows, left_norms, right_rows, right_norms):
    dot_values = lax.dot_general(
        left_rows, right_rows, (((1,), (1,)), ((), ())), preferred_element_type=jnp.float32
    )
    distance = left_norms[:, None] + right_norms[None, :] - 2.0 * dot_values
    return SIGNAL * jnp.exp(-distance / left_rows.shape[1])


def kernel_apply(left_rows, left_norms, right_rows, right_norms, weights):
    kernel_tile = kernel_tile_of(left_rows, left_norms, right_rows, right_norms)
    return jnp.dot(kernel_tile, weights, precision=lax.Precision.HIGH)


def prior_values(cand_rows, frequencies, phases, prior_weight):
    angles = (
        jnp.dot(cand_rows, frequencies, preferred_element_type=jnp.float32) * math.sqrt(2.0)
        + phases[None, :]
    )
    features = math.sqrt(2.0 * SIGNAL / frequencies.shape[1]) * jnp.cos(angles)
    return jnp.dot(features, prior_weight, precision=lax.Precision.HIGHEST)


def gather_blocks(block, axis):
    length = lax.axis_size(axis)
    flat = block.reshape(1, -1)
    spread = jnp.broadcast_to(flat, (length, flat.shape[1]))
    got = lax.all_to_all(spread, axis, 0, 0, tiled=True)
    return got.reshape((length,) + block.shape)


def gather_stack(block, axis):
    length = lax.axis_size(axis)
    spread = jnp.broadcast_to(block[None], (length,) + block.shape)
    return lax.all_to_all(spread, axis, 0, 0, tiled=True)


def gather_by_permutes(block, axis):
    length = lax.axis_size(axis)
    here = lax.axis_index(axis)
    moved = [block] + [passed_along(block, axis, by) for by in range(1, length)]
    order = (here - jnp.arange(length, dtype=jnp.int32)) % length
    return jnp.take(jnp.stack(moved), order, axis=0)


def sum_to_owners(partial, axis):
    length = lax.axis_size(axis)
    flat = partial.reshape(length, -1)
    got = lax.all_to_all(flat, axis, 0, 0, tiled=True)
    return jnp.sum(got, axis=0).reshape(partial.shape[1:])


def velocity_weights(steps):
    a, b = [], []
    for t in range(steps):
        a.append(sum(MOMENTUM ** u for u in range(1, t + 1)))
        b.append([sum(MOMENTUM ** (u - 1 - s) for u in range(s + 1, t + 1)) for s in range(t)])
    return a, b


def shards(
    records,
    coefficients,
    velocity,
    targets,
    block_local,
    block_count,
    candidates,
    frequencies,
    phases,
    prior_weight,
):
    n_blk = lax.axis_size("blk")
    record_total = records.shape[0] * n_blk
    root_count = jnp.sqrt(jnp.float32(record_total))
    steps, slot_count = block_local.shape
    own_index = lax.axis_index("blk")
    work_norms = square_norms(records)
    slot_ids = jnp.arange(slot_count, dtype=jnp.int32)
    paths = coefficients.shape[1]

    n_path = lax.axis_size("path")
    path_index = lax.axis_index("path")
    share = slot_count // n_path
    own_rows = records[block_local.reshape(-1)]
    prior = prior_values(candidates, frequencies, phases, prior_weight)

    share_local = lax.dynamic_slice_in_dim(block_local, path_index * share, share, axis=1)
    share_rows = records[share_local.reshape(-1)]
    gathered = gather_stack(share_rows, "blk")
    gathered, prior = lax.optimization_barrier((gathered, prior))
    all_rows = gathered.reshape(n_blk * steps * share, -1)
    start_weights = jnp.concatenate([coefficients, velocity], axis=1)
    every_weights = gather_by_permutes(start_weights, "path").transpose(1, 0, 2)
    every_weights = every_weights.reshape(start_weights.shape[0], n_path * 2 * paths)
    partial = kernel_apply(all_rows, square_norms(all_rows), records, work_norms, every_weights)
    partial, late_candidates = lax.optimization_barrier((partial, candidates))
    neighbour = passed_along(late_candidates, "blk", 1)
    share_sums = sum_to_owners(partial.reshape(n_blk, steps * share, n_path * 2 * paths), "blk")
    share_sums = share_sums.reshape(steps * share, n_path, 2 * paths).transpose(1, 0, 2)
    got = lax.all_to_all(share_sums, "path", 0, 0, tiled=True)
    start_sums = got.reshape(n_path, steps, share, 2 * paths).transpose(1, 0, 2, 3)
    start_sums = start_sums.reshape(steps, slot_count, 2 * paths)

    pairs = [(t, s) for t in range(steps) for s in range(t)]
    tiles = []
    for t, s in pairs:
        mine = own_rows[t * slot_count:(t + 1) * slot_count]
        theirs = gathered[:, s * share:(s + 1) * share].reshape(n_blk * share, -1)
        tiles.append(kernel_tile_of(mine, square_norms(mine), theirs, square_norms(theirs)))
    tiles = gather_by_permutes(jnp.stack(tiles), "path")
    tile_of = {pair: tiles[:, k] for k, pair in enumerate(pairs)}

    neighbour, _ = lax.optimization_barrier((neighbour, start_sums))
    a_weight, b_weight = velocity_weights(steps + 1)
    own_rows_norms = square_norms(own_rows)
    cand_norms = square_norms(candidates)
    neighbour_norms = square_norms(neighbour)
    own_start = kernel_apply(candidates, cand_norms, records, work_norms, start_weights)
    next_start = kernel_apply(neighbour, neighbour_norms, records, work_norms, start_weights)
    own_slots = kernel_tile_of(candidates, cand_norms, own_rows, own_rows_norms)
    next_slots = kernel_tile_of(neighbour, neighbour_norms, own_rows, own_rows_norms)
    weighted_updates = []
    updates = []
    for repeat in range(steps):
        local_rows = block_local[repeat]
        own_count = lax.dynamic_index_in_dim(block_count[repeat], own_index, 0, keepdims=False)
        is_live = slot_ids < own_count
        total = start_sums[repeat, :, :paths]
        if repeat > 0:
            total = total + a_weight[repeat] * start_sums[repeat, :, paths:]
        for earlier in range(repeat):
            cross = lax.dot_general(
                tile_of[(repeat, earlier)],
                updates[earlier],
                (((0, 2), (0, 1)), ((), ())),
                precision=lax.Precision.HIGH,
            )
            total = total + b_weight[repeat][earlier] * cross
        product = total / root_count
        gradient = jnp.where(
            is_live[:, None], product + NOISE * coefficients[local_rows] - targets[local_rows], 0.0
        )
        step_update = -RATE * gradient
        velocity = (MOMENTUM * velocity).at[local_rows].add(step_update)
        coefficients = coefficients + velocity
        weighted_updates.append(b_weight[steps][repeat] * step_update)
        if repeat < steps - 1:
            every_update = gather_blocks(step_update, "blk").reshape(n_blk, n_path, share, paths)
            every_update = every_update.transpose(1, 0, 2, 3).reshape(n_path, n_blk * share, paths)
            updates.append(every_update)

    slot_weights = jnp.concatenate(weighted_updates, axis=0)
    own_sum = (
        own_start[:, :paths]
        + a_weight[steps] * own_start[:, paths:]
        + jnp.dot(own_slots, slot_weights, precision=lax.Precision.HIGH)
    )
    next_sum = (
        next_start[:, :paths]
        + a_weight[steps] * next_start[:, paths:]
        + jnp.dot(next_slots, slot_weights, precision=lax.Precision.HIGH)
    )
    first_part = prior + own_sum / root_count
    next_term = next_sum / root_count
    scores = passed_along(first_part, "blk", 2) + passed_along(next_term, "blk", 1)
    squares_local = jnp.sum(scores * scores, axis=1)
    summed = lax.psum(squares_local, "path")
    path_rms = jnp.sqrt(summed / (scores.shape[1] * lax.axis_size("path")) + EPSILON)
    return (coefficients, velocity, scores, path_rms)


def solution(mesh):
    return jax.shard_map(
        shards,
        mesh=mesh,
        in_specs=(
            P("blk", None),
            P("blk", "path"),
            P("blk", "path"),
            P("blk", "path"),
            P(None, "blk"),
            P(),
            P("blk", None),
            P(),
            P(),
            P(None, "path"),
        ),
        out_specs=(P("blk", "path"), P("blk", "path"), P("blk", "path"), P("blk")),
        check_vma=False,
    )
```

```python
import math

import jax
import jax.numpy as jnp
from jax import lax
from jax.sharding import PartitionSpec as P

NOISE = 0.5
MOMENTUM = 0.9
RATE = 0.3
EPSILON = 1e-06
SIGNAL = 9.0


def passed_along(shard, axis, by):
    length = lax.axis_size(axis)
    return lax.ppermute(shard, axis, [(i, (i + by) % length) for i in range(length)])


def square_norms(row_block):
    widened = row_block.astype(jnp.float32)
    return jnp.sum(widened * widened, axis=1)


def kernel_tile_of(left_rows, left_norms, right_rows, right_norms):
    dot_values = lax.dot_general(
        left_rows, right_rows, (((1,), (1,)), ((), ())), preferred_element_type=jnp.float32
    )
    distance = left_norms[:, None] + right_norms[None, :] - 2.0 * dot_values
    return SIGNAL * jnp.exp(-distance / left_rows.shape[1])


def kernel_apply(left_rows, left_norms, right_rows, right_norms, weights):
    kernel_tile = kernel_tile_of(left_rows, left_norms, right_rows, right_norms)
    return jnp.dot(kernel_tile, weights, precision=lax.Precision.HIGH)


def prior_values(cand_rows, frequencies, phases, prior_weight):
    angles = (
        jnp.dot(cand_rows, frequencies, preferred_element_type=jnp.float32) * math.sqrt(2.0)
        + phases[None, :]
    )
    features = math.sqrt(2.0 * SIGNAL / frequencies.shape[1]) * jnp.cos(angles)
    return jnp.dot(features, prior_weight, precision=lax.Precision.HIGHEST)


def gather_blocks(block, axis):
    length = lax.axis_size(axis)
    flat = block.reshape(1, -1)
    spread = jnp.broadcast_to(flat, (length, flat.shape[1]))
    got = lax.all_to_all(spread, axis, 0, 0, tiled=True)
    return got.reshape((length,) + block.shape)


def gather_stack(block, axis):
    length = lax.axis_size(axis)
    spread = jnp.broadcast_to(block[None], (length,) + block.shape)
    return lax.all_to_all(spread, axis, 0, 0, tiled=True)


def gather_by_permutes(block, axis):
    length = lax.axis_size(axis)
    here = lax.axis_index(axis)
    moved = [block] + [passed_along(block, axis, by) for by in range(1, length)]
    order = (here - jnp.arange(length, dtype=jnp.int32)) % length
    return jnp.take(jnp.stack(moved), order, axis=0)


def sum_to_owners(partial, axis):
    length = lax.axis_size(axis)
    flat = partial.reshape(length, -1)
    got = lax.all_to_all(flat, axis, 0, 0, tiled=True)
    return jnp.sum(got, axis=0).reshape(partial.shape[1:])


def velocity_weights(steps):
    a, b = [], []
    for t in range(steps):
        a.append(sum(MOMENTUM ** u for u in range(1, t + 1)))
        b.append([sum(MOMENTUM ** (u - 1 - s) for u in range(s + 1, t + 1)) for s in range(t)])
    return a, b


def shards(
    records,
    coefficients,
    velocity,
    targets,
    block_local,
    block_count,
    candidates,
    frequencies,
    phases,
    prior_weight,
):
    n_blk = lax.axis_size("blk")
    record_total = records.shape[0] * n_blk
    root_count = jnp.sqrt(jnp.float32(record_total))
    steps, slot_count = block_local.shape
    own_index = lax.axis_index("blk")
    work_norms = square_norms(records)
    slot_ids = jnp.arange(slot_count, dtype=jnp.int32)
    paths = coefficients.shape[1]

    n_path = lax.axis_size("path")
    path_index = lax.axis_index("path")
    share = slot_count // n_path
    own_rows = records[block_local.reshape(-1)]
    prior = prior_values(candidates, frequencies, phases, prior_weight)

    share_local = lax.dynamic_slice_in_dim(block_local, path_index * share, share, axis=1)
    share_rows = records[share_local.reshape(-1)]
    gathered = gather_stack(share_rows, "blk")
    gathered, prior = lax.optimization_barrier((gathered, prior))
    all_rows = gathered.reshape(n_blk * steps * share, -1)
    start_weights = jnp.concatenate([coefficients, velocity], axis=1)
    every_weights = gather_by_permutes(start_weights, "path").transpose(1, 0, 2)
    every_weights = every_weights.reshape(start_weights.shape[0], n_path * 2 * paths)
    partial = kernel_apply(all_rows, square_norms(all_rows), records, work_norms, every_weights)
    partial, late_candidates = lax.optimization_barrier((partial, candidates))
    neighbour = passed_along(late_candidates, "blk", 1)
    share_sums = sum_to_owners(partial.reshape(n_blk, steps * share, n_path * 2 * paths), "blk")
    share_sums = share_sums.reshape(steps * share, n_path, 2 * paths).transpose(1, 0, 2)
    got = lax.all_to_all(share_sums, "path", 0, 0, tiled=True)
    start_sums = got.reshape(n_path, steps, share, 2 * paths).transpose(1, 0, 2, 3)
    start_sums = start_sums.reshape(steps, slot_count, 2 * paths)

    pairs = [(t, s) for t in range(steps) for s in range(t)]
    tiles = []
    for t, s in pairs:
        mine = own_rows[t * slot_count:(t + 1) * slot_count]
        theirs = gathered[:, s * share:(s + 1) * share].reshape(n_blk * share, -1)
        tiles.append(kernel_tile_of(mine, square_norms(mine), theirs, square_norms(theirs)))
    tiles = gather_by_permutes(jnp.stack(tiles), "path")
    tile_of = {pair: tiles[:, k] for k, pair in enumerate(pairs)}

    neighbour, _ = lax.optimization_barrier((neighbour, start_sums))
    a_weight, b_weight = velocity_weights(steps + 1)
    own_rows_norms = square_norms(own_rows)
    cand_norms = square_norms(candidates)
    neighbour_norms = square_norms(neighbour)
    own_start = kernel_apply(candidates, cand_norms, records, work_norms, start_weights)
    next_start = kernel_apply(neighbour, neighbour_norms, records, work_norms, start_weights)
    own_slots = kernel_tile_of(candidates, cand_norms, own_rows, own_rows_norms)
    next_slots = kernel_tile_of(neighbour, neighbour_norms, own_rows, own_rows_norms)
    weighted_updates = []
    updates = []
    for repeat in range(steps):
        local_rows = block_local[repeat]
        own_count = lax.dynamic_index_in_dim(block_count[repeat], own_index, 0, keepdims=False)
        is_live = slot_ids < own_count
        total = start_sums[repeat, :, :paths]
        if repeat > 0:
            total = total + a_weight[repeat] * start_sums[repeat, :, paths:]
        for earlier in range(repeat):
            cross = lax.dot_general(
                tile_of[(repeat, earlier)],
                updates[earlier],
                (((0, 2), (0, 1)), ((), ())),
                precision=lax.Precision.HIGH,
            )
            total = total + b_weight[repeat][earlier] * cross
        product = total / root_count
        gradient = jnp.where(
            is_live[:, None], product + NOISE * coefficients[local_rows] - targets[local_rows], 0.0
        )
        step_update = -RATE * gradient
        velocity = (MOMENTUM * velocity).at[local_rows].add(step_update)
        coefficients = coefficients + velocity
        weighted_updates.append(b_weight[steps][repeat] * step_update)
        if repeat < steps - 1:
            every_update = gather_blocks(step_update, "blk").reshape(n_blk, n_path, share, paths)
            every_update = every_update.transpose(1, 0, 2, 3).reshape(n_path, n_blk * share, paths)
            updates.append(every_update)

    slot_weights = jnp.concatenate(weighted_updates, axis=0)
    own_sum = (
        own_start[:, :paths]
        + a_weight[steps] * own_start[:, paths:]
        + jnp.dot(own_slots, slot_weights, precision=lax.Precision.HIGH)
    )
    next_sum = (
        next_start[:, :paths]
        + a_weight[steps] * next_start[:, paths:]
        + jnp.dot(next_slots, slot_weights, precision=lax.Precision.HIGH)
    )
    first_part = prior + own_sum / root_count
    next_term = next_sum / root_count
    scores = passed_along(first_part, "blk", 2) + passed_along(next_term, "blk", 1)
    squares_local = jnp.sum(scores * scores, axis=1)
    summed = jnp.sum(gather_blocks(squares_local, "path"), axis=0)
    path_rms = jnp.sqrt(summed / (scores.shape[1] * lax.axis_size("path")) + EPSILON)
    return (coefficients, velocity, scores, path_rms)


def solution(mesh):
    return jax.shard_map(
        shards,
        mesh=mesh,
        in_specs=(
            P("blk", None),
            P("blk", "path"),
            P("blk", "path"),
            P("blk", "path"),
            P(None, "blk"),
            P(),
            P("blk", None),
            P(),
            P(),
            P(None, "path"),
        ),
        out_specs=(P("blk", "path"), P("blk", "path"), P("blk", "path"), P("blk")),
        check_vma=False,
    )
```

```python
import math

import jax
import jax.numpy as jnp
from jax import lax
from jax.sharding import PartitionSpec as P

NOISE = 0.5
MOMENTUM = 0.9
RATE = 0.3
EPSILON = 1e-06
SIGNAL = 9.0


def passed_along(shard, axis, by):
    length = lax.axis_size(axis)
    return lax.ppermute(shard, axis, [(i, (i + by) % length) for i in range(length)])


def square_norms(row_block):
    widened = row_block.astype(jnp.float32)
    return jnp.sum(widened * widened, axis=1)


def kernel_tile_of(left_rows, left_norms, right_rows, right_norms):
    dot_values = lax.dot_general(
        left_rows, right_rows, (((1,), (1,)), ((), ())), preferred_element_type=jnp.float32
    )
    distance = left_norms[:, None] + right_norms[None, :] - 2.0 * dot_values
    return SIGNAL * jnp.exp(-distance / left_rows.shape[1])


def kernel_apply(left_rows, left_norms, right_rows, right_norms, weights):
    kernel_tile = kernel_tile_of(left_rows, left_norms, right_rows, right_norms)
    return jnp.dot(kernel_tile, weights, precision=lax.Precision.HIGH)


def prior_values(cand_rows, frequencies, phases, prior_weight):
    angles = (
        jnp.dot(cand_rows, frequencies, preferred_element_type=jnp.float32) * math.sqrt(2.0)
        + phases[None, :]
    )
    features = math.sqrt(2.0 * SIGNAL / frequencies.shape[1]) * jnp.cos(angles)
    return jnp.dot(features, prior_weight, precision=lax.Precision.HIGHEST)


def gather_blocks(block, axis):
    length = lax.axis_size(axis)
    flat = block.reshape(1, -1)
    spread = jnp.broadcast_to(flat, (length, flat.shape[1]))
    got = lax.all_to_all(spread, axis, 0, 0, tiled=True)
    return got.reshape((length,) + block.shape)


def gather_stack(block, axis):
    length = lax.axis_size(axis)
    spread = jnp.broadcast_to(block[None], (length,) + block.shape)
    return lax.all_to_all(spread, axis, 0, 0, tiled=True)


def gather_by_permutes(block, axis):
    length = lax.axis_size(axis)
    here = lax.axis_index(axis)
    moved = [block] + [passed_along(block, axis, by) for by in range(1, length)]
    order = (here - jnp.arange(length, dtype=jnp.int32)) % length
    return jnp.take(jnp.stack(moved), order, axis=0)


def sum_to_owners(partial, axis):
    length = lax.axis_size(axis)
    flat = partial.reshape(length, -1)
    got = lax.all_to_all(flat, axis, 0, 0, tiled=True)
    return jnp.sum(got, axis=0).reshape(partial.shape[1:])


def velocity_weights(steps):
    a, b = [], []
    for t in range(steps):
        a.append(sum(MOMENTUM ** u for u in range(1, t + 1)))
        b.append([sum(MOMENTUM ** (u - 1 - s) for u in range(s + 1, t + 1)) for s in range(t)])
    return a, b


def shards(
    records,
    coefficients,
    velocity,
    targets,
    block_local,
    block_count,
    candidates,
    frequencies,
    phases,
    prior_weight,
):
    n_blk = lax.axis_size("blk")
    record_total = records.shape[0] * n_blk
    root_count = jnp.sqrt(jnp.float32(record_total))
    steps, slot_count = block_local.shape
    own_index = lax.axis_index("blk")
    work_norms = square_norms(records)
    slot_ids = jnp.arange(slot_count, dtype=jnp.int32)
    paths = coefficients.shape[1]

    n_path = lax.axis_size("path")
    path_index = lax.axis_index("path")
    share = slot_count // n_path
    own_rows = records[block_local.reshape(-1)]
    prior = prior_values(candidates, frequencies, phases, prior_weight)

    share_local = lax.dynamic_slice_in_dim(block_local, path_index * share, share, axis=1)
    share_rows = records[share_local.reshape(-1)]
    gathered = gather_stack(share_rows, "blk")
    gathered, prior = lax.optimization_barrier((gathered, prior))
    all_rows = gathered.reshape(n_blk * steps * share, -1)
    start_weights = jnp.concatenate([coefficients, velocity], axis=1)
    every_weights = gather_by_permutes(start_weights, "path").transpose(1, 0, 2)
    every_weights = every_weights.reshape(start_weights.shape[0], n_path * 2 * paths)
    partial = kernel_apply(all_rows, square_norms(all_rows), records, work_norms, every_weights)
    partial, late_candidates = lax.optimization_barrier((partial, candidates))
    neighbour = passed_along(late_candidates, "blk", 1)
    share_sums = sum_to_owners(partial.reshape(n_blk, steps * share, n_path * 2 * paths), "blk")
    share_sums = share_sums.reshape(steps * share, n_path, 2 * paths).transpose(1, 0, 2)
    got = lax.all_to_all(share_sums, "path", 0, 0, tiled=True)
    start_sums = got.reshape(n_path, steps, share, 2 * paths).transpose(1, 0, 2, 3)
    start_sums = start_sums.reshape(steps, slot_count, 2 * paths)

    pairs = [(t, s) for t in range(steps) for s in range(t)]
    tiles = []
    for t, s in pairs:
        mine = own_rows[t * slot_count:(t + 1) * slot_count]
        theirs = gathered[:, s * share:(s + 1) * share].reshape(n_blk * share, -1)
        tiles.append(kernel_tile_of(mine, square_norms(mine), theirs, square_norms(theirs)))
    tiles, _ = lax.optimization_barrier((jnp.stack(tiles), start_sums))
    tiles = gather_by_permutes(tiles, "path")
    tile_of = {pair: tiles[:, k] for k, pair in enumerate(pairs)}

    neighbour, _ = lax.optimization_barrier((neighbour, start_sums))
    a_weight, b_weight = velocity_weights(steps + 1)
    own_rows_norms = square_norms(own_rows)
    cand_norms = square_norms(candidates)
    neighbour_norms = square_norms(neighbour)
    own_start = kernel_apply(candidates, cand_norms, records, work_norms, start_weights)
    next_start = kernel_apply(neighbour, neighbour_norms, records, work_norms, start_weights)
    own_slots = kernel_tile_of(candidates, cand_norms, own_rows, own_rows_norms)
    next_slots = kernel_tile_of(neighbour, neighbour_norms, own_rows, own_rows_norms)
    weighted_updates = []
    updates = []
    for repeat in range(steps):
        local_rows = block_local[repeat]
        own_count = lax.dynamic_index_in_dim(block_count[repeat], own_index, 0, keepdims=False)
        is_live = slot_ids < own_count
        total = start_sums[repeat, :, :paths]
        if repeat > 0:
            total = total + a_weight[repeat] * start_sums[repeat, :, paths:]
        for earlier in range(repeat):
            cross = lax.dot_general(
                tile_of[(repeat, earlier)],
                updates[earlier],
                (((0, 2), (0, 1)), ((), ())),
                precision=lax.Precision.HIGH,
            )
            total = total + b_weight[repeat][earlier] * cross
        product = total / root_count
        gradient = jnp.where(
            is_live[:, None], product + NOISE * coefficients[local_rows] - targets[local_rows], 0.0
        )
        step_update = -RATE * gradient
        velocity = (MOMENTUM * velocity).at[local_rows].add(step_update)
        coefficients = coefficients + velocity
        weighted_updates.append(b_weight[steps][repeat] * step_update)
        if repeat < steps - 1:
            every_update = gather_blocks(step_update, "blk").reshape(n_blk, n_path, share, paths)
            every_update = every_update.transpose(1, 0, 2, 3).reshape(n_path, n_blk * share, paths)
            updates.append(every_update)

    slot_weights = jnp.concatenate(weighted_updates, axis=0)
    own_sum = (
        own_start[:, :paths]
        + a_weight[steps] * own_start[:, paths:]
        + jnp.dot(own_slots, slot_weights, precision=lax.Precision.HIGH)
    )
    next_sum = (
        next_start[:, :paths]
        + a_weight[steps] * next_start[:, paths:]
        + jnp.dot(next_slots, slot_weights, precision=lax.Precision.HIGH)
    )
    first_part = prior + own_sum / root_count
    next_term = next_sum / root_count
    scores = passed_along(first_part, "blk", 2) + passed_along(next_term, "blk", 1)
    squares_local = jnp.sum(scores * scores, axis=1)
    summed = jnp.sum(gather_blocks(squares_local, "path"), axis=0)
    path_rms = jnp.sqrt(summed / (scores.shape[1] * lax.axis_size("path")) + EPSILON)
    return (coefficients, velocity, scores, path_rms)


def solution(mesh):
    return jax.shard_map(
        shards,
        mesh=mesh,
        in_specs=(
            P("blk", None),
            P("blk", "path"),
            P("blk", "path"),
            P("blk", "path"),
            P(None, "blk"),
            P(),
            P("blk", None),
            P(),
            P(),
            P(None, "path"),
        ),
        out_specs=(P("blk", "path"), P("blk", "path"), P("blk", "path"), P("blk")),
        check_vma=False,
    )
```
